32 devices in a mesh: front: 2 (over x), column: 4 (over y, core), row: 4 (over z).
Axes of the slice: x: 2, y: 2, z: 4, core: 2. Of those that a mesh axis runs over, the one named last changes fastest.
Arguments:
- cbs: float32 [2, 2, 2048, 2048], P('front', None, 'row', 'column'), may hold values from -4 to 4
- row_map: int32 [2, 2, 16], P('front'), may hold values from 0 to 47, as said below
- col_map: int32 [2, 2, 16], P('front'), may hold values from 0 to 47, as said below
- child_size: int32 [2, 2], P('front'), may hold values from 8 to 16, as said below
- front_diag: float32 [2, 6144], P('front'), may hold values from 0.1 to 200
- panel_order: int32 [2, 4], P('front'), may hold values from 0 to 23, as said below
- pivot_inverse: float32 [2, 4, 256, 256], P('front'), may hold values from -0.2 to 0.8
Outputs:
- factored_front: float32 [2, 6144, 6144], P('front', 'row', 'column')
The draws below stay inside these ranges and needn't reach their ends.
Inputs may be any that keep to these rules, and one draw needn't show every extreme that they name: `row_map`: entries of one child are distinct. Split the parent tiles into aligned runs of 12 consecutive tiles (tiles t with the same t // 12, the tiles one row owner holds). In each aligned run of 4 entries at most 2 lie in one such aligned parent run, and in every aligned run of 4 entries some aligned parent run gets exactly 2. `col_map`: entries of one child are distinct. Split the parent tiles into aligned runs of 12 consecutive tiles (tiles t with the same t // 12, the tiles one column owner holds). In each aligned run of 4 entries no two lie in the same such aligned parent run. `child_size`: every front has a child of size 16. `panel_order`: distinct within a front. The first and the last panel block are each eliminated by exactly one front.
All inputs are finite; a program needn't handle non-finite values.
Results may differ from the reference program's by a relative error of at most 0.0003.
Values sent between devices are 32-bit elements; how exact they have to be, the bound alone decides.
No kernel may reach another device: no remote copies, remote signals or barrier semaphores. Data moves between devices by JAX's collectives and lax.ppermute only.
A program may use at most 192 MiB of HBM per device.

```python
import math
import jax
import jax.numpy as jnp
from jax import lax

ORDER = 6144
TILE = 128
PANEL = 256
PANELS = 4
MAXB = 16
ROWMOST = 2
FRONTS = 2
N_FRONT = 2
N_COLUMN = 4
N_ROW = 4


def child_maps(key, owners, limit_per):
    seg_len = MAXB // owners
    per_owner = ORDER // TILE // owners
    child_count = N_FRONT * FRONTS
    seg_keys = jax.random.split(jax.random.fold_in(key, 1), child_count * owners)

    def one_segment(seg_key):
        key_lead, key_rest, key_order = jax.random.split(seg_key, 3)
        lead_owner = jax.random.randint(key_lead, (), 0, owners)
        others = (lead_owner + 1 + jnp.arange((owners - 1) * limit_per, dtype=jnp.int32) // limit_per) % owners
        others = jax.random.permutation(key_rest, others)
        sequence = jnp.concatenate([jnp.full((limit_per,), lead_owner, jnp.int32), others[:seg_len - limit_per]])
        return jax.random.permutation(key_order, sequence)
    owner_seq = jax.vmap(one_segment)(seg_keys).reshape(child_count, MAXB).astype(jnp.int32)
    same_owner = (owner_seq[:, :, None] == owner_seq[:, None, :]).astype(jnp.int32)
    strict_lower = jnp.tril(jnp.ones((MAXB, MAXB), jnp.int32), -1)
    local_rank = jnp.sum(same_owner * strict_lower[None, :, :], axis=2)
    shuffle_keys = jax.random.split(jax.random.fold_in(key, 2), child_count * owners)

    def one_shuffle(shuffle_key):
        return jax.random.permutation(shuffle_key, per_owner).astype(jnp.int32)
    shuffles = jax.vmap(one_shuffle)(shuffle_keys).reshape(child_count, owners, per_owner)
    picked_rows = jnp.take_along_axis(shuffles, owner_seq[:, :, None], axis=1)
    chosen_local = jnp.take_along_axis(picked_rows, local_rank[:, :, None], axis=2)[:, :, 0]
    return (owner_seq * per_owner + chosen_local).reshape(N_FRONT, FRONTS, MAXB).astype(jnp.int32)


def draw_row_map(key, part):
    return child_maps(jax.random.fold_in(key, 11), N_ROW, ROWMOST)


def draw_col_map(key, part):
    return child_maps(jax.random.fold_in(key, 12), N_COLUMN, 1)


def draw_child_size(key, part):
    key_sizes = jax.random.fold_in(key, 21)
    key_full = jax.random.fold_in(key, 22)
    drawn_sizes = jax.random.randint(key_sizes, (N_FRONT, FRONTS), MAXB // 2, MAXB + 1)
    full_child = jax.random.randint(key_full, (FRONTS,), 0, N_FRONT)
    group_iota = jnp.arange(N_FRONT, dtype=jnp.int32)
    return jnp.where(group_iota[:, None] == full_child[None, :], MAXB, drawn_sizes).astype(jnp.int32)


def draw_front_diag(key, part):
    key_vals = jax.random.fold_in(key, 51)
    log_vals = jax.random.uniform(key_vals, (FRONTS, ORDER), jnp.float32, math.log(0.2), math.log(100.0))
    return jnp.clip(jnp.exp(log_vals), 0.1, 200.0).astype(jnp.float32)


def draw_panel_order(key, part):
    block_count = ORDER // PANEL
    order_keys = jax.random.split(jax.random.fold_in(key, 31), FRONTS)

    def one_order(order_key):
        return jax.random.permutation(order_key, block_count - 2)[:PANELS] + 1
    inner = jax.vmap(one_order)(order_keys).astype(jnp.int32)
    top_front = jax.random.randint(jax.random.fold_in(key, 32), (), 0, FRONTS)
    top_spot = jax.random.randint(jax.random.fold_in(key, 33), (), 0, PANELS)
    low_front = jax.random.randint(jax.random.fold_in(key, 34), (), 0, FRONTS)
    low_drawn = jax.random.randint(jax.random.fold_in(key, 35), (), 0, PANELS)
    low_spot = jnp.where(low_front == top_front, (top_spot + 1) % PANELS, low_drawn)
    front_iota = jnp.arange(FRONTS, dtype=jnp.int32)[:, None]
    spot_iota = jnp.arange(PANELS, dtype=jnp.int32)[None, :]
    inner = jnp.where((front_iota == top_front) & (spot_iota == top_spot), block_count - 1, inner)
    inner = jnp.where((front_iota == low_front) & (spot_iota == low_spot), 0, inner)
    return inner.astype(jnp.int32)


def draw_pivot_inverse(key, part):
    key_diag = jax.random.fold_in(key, 41)
    key_off = jax.random.fold_in(key, 42)
    diag_vals = jnp.exp(jax.random.uniform(key_diag, (FRONTS, PANELS, PANEL), jnp.float32, math.log(0.2), math.log(0.5)))
    off_vals = jnp.clip(jax.random.normal(key_off, (FRONTS, PANELS, PANEL, PANEL), jnp.float32), -4.0, 4.0)
    identity_mat = jnp.eye(PANEL, dtype=jnp.float32)
    return (identity_mat * diag_vals[..., None] + 0.12 / math.sqrt(PANEL) * off_vals).astype(jnp.float32)


def levels(own_key, shape, cuts, smallest, high):
    loudness = 1.0
    for dim, blocks in cuts:
        draws = jax.random.uniform(jax.random.fold_in(jax.random.fold_in(own_key, 6), dim), (blocks,), jnp.float32, smallest / len(cuts), high / len(cuts))
        loudness = loudness * jnp.repeat(jnp.exp(draws), shape[dim] // blocks).reshape((-1,) + (1,) * (len(shape) - 1 - dim))
    return loudness


def gaussian(own_key, shape, spread, limit, shards=(), kind=jnp.bfloat16):
    drawn = jax.random.normal(own_key, shape, jnp.float32) * spread
    if len(shards) > 0:
        drawn = levels(own_key, shape, shards, -0.22, 0.18) * drawn
    return jnp.clip(drawn, min=-limit, max=limit).astype(kind)


def setup_inputs(seed: int = 0) -> dict:
    keys = jax.random.split(jax.random.key(seed), 8)
    cbs = gaussian(keys[0], (N_FRONT, FRONTS, MAXB * TILE, MAXB * TILE), 0.3, 4.0, ((0, 2), (2, 4), (3, 4)), jnp.float32)
    row_map = draw_row_map(jax.random.fold_in(keys[7], 71), 0)
    col_map = draw_col_map(jax.random.fold_in(keys[7], 71), 0)
    child_size = draw_child_size(jax.random.fold_in(keys[7], 71), 0)
    front_diag = draw_front_diag(jax.random.fold_in(keys[7], 71), 0)
    panel_order = draw_panel_order(jax.random.fold_in(keys[7], 71), 0)
    pivot_inverse = draw_pivot_inverse(jax.random.fold_in(keys[7], 71), 0)
    return dict(cbs=cbs, row_map=row_map, col_map=col_map, child_size=child_size, front_diag=front_diag, panel_order=panel_order, pivot_inverse=pivot_inverse)


HIGHEST = lax.Precision.HIGHEST


def assemble(front_id, cbs, row_map, col_map, child_size, front_diag):
    blocks_side = ORDER // TILE
    start_grid = jnp.zeros((blocks_side, blocks_side, TILE, TILE), jnp.float32)

    def add_child(tile_grid, group_id):
        child_tiles = cbs[group_id, front_id].reshape(MAXB, TILE, MAXB, TILE).transpose(0, 2, 1, 3)
        child_len = child_size[group_id, front_id]
        live_idx = jnp.arange(MAXB, dtype=jnp.int32) < child_len
        live_pair = live_idx[:, None] & live_idx[None, :]
        child_tiles = jnp.where(live_pair[:, :, None, None], child_tiles, 0.0)
        dest_rows = row_map[group_id, front_id]
        dest_cols = col_map[group_id, front_id]
        tile_grid = tile_grid.at[dest_rows[:, None], dest_cols[None, :]].add(child_tiles)
        return tile_grid, None

    tile_grid, _ = lax.scan(add_child, start_grid, jnp.arange(N_FRONT, dtype=jnp.int32))
    matrix = tile_grid.transpose(0, 2, 1, 3).reshape(ORDER, ORDER)
    return matrix + jnp.diag(front_diag[front_id])


def factor(matrix, order_row, inverses):
    block_of = jnp.arange(ORDER, dtype=jnp.int32) // PANEL
    for step_index in range(PANELS):
        pivot_block = order_row[step_index]
        chosen = order_row[: step_index + 1]
        active = jnp.all(block_of[:, None] != chosen[None, :], axis=1)
        start_col = pivot_block * PANEL
        col_strip = lax.dynamic_slice_in_dim(matrix, start_col, PANEL, 1)
        row_strip = lax.dynamic_slice_in_dim(matrix, start_col, PANEL, 0)
        left_factor = jnp.dot(col_strip, inverses[step_index], precision=HIGHEST, preferred_element_type=jnp.float32)
        product = jnp.dot(left_factor, row_strip, precision=HIGHEST, preferred_element_type=jnp.float32)
        matrix = jnp.where(active[:, None] & active[None, :], matrix - product, matrix)
        present = lax.dynamic_slice_in_dim(matrix, start_col, PANEL, 1)
        matrix = lax.dynamic_update_slice_in_dim(matrix, jnp.where(active[:, None], left_factor, present), start_col, 1)
    return matrix


def reference(cbs, row_map, col_map, child_size, front_diag, panel_order, pivot_inverse):
    def one_front(front_id):
        matrix = assemble(front_id, cbs, row_map, col_map, child_size, front_diag)
        return factor(matrix, panel_order[front_id], pivot_inverse[front_id])

    return lax.map(one_front, jnp.arange(FRONTS, dtype=jnp.int32))
```

```python
import jax
import jax.numpy as jnp
from jax import lax
from jax.sharding import PartitionSpec as P

ORDER = 6144
TILE = 128
PANEL = 256
PANELS = 4
ROWMOST = 2


HIGHEST = lax.Precision.HIGHEST


def broadcast(block, axis, source):
    block = jnp.where(lax.axis_index(axis) == source, block, jnp.zeros_like(block))
    return lax.psum(block, axis)


def exchange_broadcast(block, axis, source):
    size = lax.axis_size(axis)
    if size & (size - 1):
        return broadcast(block, axis, source)
    index = lax.axis_index(axis)
    distance = 1
    while distance < size:
        partner = [(i, i ^ distance) for i in range(size)]
        received = lax.ppermute(block, axis, partner)
        take = (source // distance) % 2 != (index // distance) % 2
        block = jnp.where(take, received, block)
        distance *= 2
    return block


def pack_tiles(tile_stack, target_dev, target_spot, dest_count, capacity, sentinel):
    dest_iota = jnp.arange(dest_count, dtype=jnp.int32)
    matches = (target_dev[:, None] == dest_iota[None, :]).astype(jnp.int32)
    earlier = jnp.cumsum(matches, axis=0) - matches
    position = jnp.sum(earlier * matches, axis=1)
    usable = target_dev < dest_count
    slot_index = jnp.where(usable, target_dev * capacity + position, dest_count * capacity)
    payload = jnp.zeros((dest_count * capacity,) + tile_stack.shape[1:], tile_stack.dtype)
    payload = payload.at[slot_index].set(tile_stack, mode="drop")
    labels = (
        jnp.full((dest_count * capacity,), sentinel, jnp.int32)
        .at[slot_index]
        .set(target_spot, mode="drop")
    )
    return (
        payload.reshape((dest_count, capacity) + tile_stack.shape[1:]),
        labels.reshape(dest_count, capacity),
    )


def scatter_tiles(payload, labels, row_tiles, col_tiles):
    tile_side = payload.shape[-1]
    tile_grid = jnp.zeros((row_tiles * col_tiles + 1, tile_side, tile_side), jnp.float32)
    tile_grid = tile_grid.at[labels.reshape(-1)].add(payload.reshape(-1, tile_side, tile_side))
    tile_grid = tile_grid[: row_tiles * col_tiles]
    tile_grid = tile_grid.reshape(row_tiles, col_tiles, tile_side, tile_side).transpose(0, 2, 1, 3)
    return tile_grid.reshape(row_tiles * tile_side, col_tiles * tile_side)


def body(cbs, row_map, col_map, child_size, front_diag, panel_order, pivot_inverse):
    groups = lax.axis_size("front")
    row_devs = lax.axis_size("row")
    col_devs = lax.axis_size("column")
    row_id = lax.axis_index("row")
    col_id = lax.axis_index("column")
    children = cbs.shape[1]
    piece_rows = cbs.shape[2] // TILE
    piece_cols = cbs.shape[3] // TILE
    local_rows = ORDER // row_devs
    local_cols = ORDER // col_devs
    row_tiles = local_rows // TILE
    col_tiles = local_cols // TILE
    sentinel = row_tiles * col_tiles
    tile_stack = (
        cbs[0].reshape(children, piece_rows, TILE, piece_cols, TILE).transpose(0, 1, 3, 2, 4)
    )
    tile_stack = tile_stack.reshape(-1, TILE, TILE)
    child_rows = row_id * piece_rows + jnp.arange(piece_rows, dtype=jnp.int32)
    child_cols = col_id * piece_cols + jnp.arange(piece_cols, dtype=jnp.int32)
    parent_rows = lax.dynamic_slice_in_dim(row_map[0], row_id * piece_rows, piece_rows, 1)
    parent_cols = lax.dynamic_slice_in_dim(col_map[0], col_id * piece_cols, piece_cols, 1)
    live_rows = child_rows[None, :] < child_size[0][:, None]
    live_cols = child_cols[None, :] < child_size[0][:, None]
    owner_rows = parent_rows // row_tiles
    owner_cols = parent_cols // col_tiles
    target_spot = (
        (parent_rows - owner_rows * row_tiles)[:, :, None] * col_tiles
        + (parent_cols - owner_cols * col_tiles)[:, None, :]
    ).reshape(-1)
    usable = (live_rows[:, :, None] & live_cols[:, None, :]).reshape(-1)
    inner_dest = (owner_cols[:, None, :] * row_devs + owner_rows[:, :, None]).reshape(-1)
    all_devices = groups * row_devs * col_devs
    front_ids = jnp.arange(children, dtype=jnp.int32)[:, None]
    whole_dest = (front_ids * (row_devs * col_devs) + inner_dest.reshape(children, -1)).reshape(-1)
    whole_target = jnp.where(usable, whole_dest, all_devices)
    payload, labels = pack_tiles(
        tile_stack, whole_target, target_spot, all_devices, ROWMOST, sentinel
    )
    arrived, arrived_labels = (
        lax.all_to_all(
            payload, ("front", "column", "row"), split_axis=0, concat_axis=0, tiled=True
        ),
        lax.all_to_all(labels, ("front", "column", "row"), split_axis=0, concat_axis=0, tiled=True),
    )
    matrix = scatter_tiles(arrived, arrived_labels, row_tiles, col_tiles)
    row_glob = row_id * local_rows + jnp.arange(local_rows, dtype=jnp.int32)
    col_glob = col_id * local_cols + jnp.arange(local_cols, dtype=jnp.int32)
    diag_part = lax.dynamic_slice_in_dim(front_diag[0], row_id * local_rows, local_rows)
    matrix = matrix + jnp.where(row_glob[:, None] == col_glob[None, :], diag_part[:, None], 0.0)
    order_row = panel_order[0]
    inverses = pivot_inverse[0]
    panel_rows = local_rows // PANEL
    panel_cols = local_cols // PANEL
    row_block = row_glob // PANEL
    col_block = col_glob // PANEL

    def strip_bounds(step_index):
        pivot_block = order_row[step_index]
        return (
            pivot_block // panel_cols,
            pivot_block // panel_rows,
            pivot_block % panel_cols * PANEL,
            pivot_block % panel_rows * PANEL,
        )

    def actives(step_index):
        chosen = order_row[: step_index + 1]
        active_rows = jnp.all(row_block[:, None] != chosen[None, :], axis=1)
        active_cols = jnp.all(col_block[:, None] != chosen[None, :], axis=1)
        return (active_rows, active_cols)

    def current_strips(matrix, step_index):
        col_owner, row_owner, col_offset, row_offset = strip_bounds(step_index)
        return (
            lax.dynamic_slice_in_dim(matrix, col_offset, PANEL, 1),
            lax.dynamic_slice_in_dim(matrix, row_offset, PANEL, 0),
        )

    def share_strips(col_strip, row_strip, step_index):
        col_owner, row_owner, col_offset, row_offset = strip_bounds(step_index)
        owner_left = jnp.dot(
            col_strip, inverses[step_index], precision=HIGHEST, preferred_element_type=jnp.float32
        )
        left_strip = exchange_broadcast(owner_left, "column", col_owner)
        top_strip = broadcast(row_strip, "row", row_owner)
        return (left_strip, top_strip)

    first_col, first_row = current_strips(matrix, 0)
    left_strip, top_strip = share_strips(first_col, first_row, 0)
    for step_index in range(PANELS):
        if step_index + 1 < PANELS:
            active_rows, active_cols = actives(step_index)
            next_col, next_row = current_strips(matrix, step_index + 1)
            col_owner, row_owner, col_offset, row_offset = strip_bounds(step_index + 1)
            top_part = lax.dynamic_slice_in_dim(top_strip, col_offset, PANEL, 1)
            left_part = lax.dynamic_slice_in_dim(left_strip, row_offset, PANEL, 0)
            next_col = jnp.where(
                active_rows[:, None],
                next_col
                - jnp.dot(
                    left_strip, top_part, precision=HIGHEST, preferred_element_type=jnp.float32
                ),
                next_col,
            )
            next_row = jnp.where(
                active_cols[None, :],
                next_row
                - jnp.dot(
                    left_part, top_strip, precision=HIGHEST, preferred_element_type=jnp.float32
                ),
                next_row,
            )
            left_next, top_next = share_strips(next_col, next_row, step_index + 1)
        eliminate_matrix = matrix
        eliminate_active_rows, eliminate_active_cols = actives(step_index)
        product = jnp.dot(
            left_strip, top_strip, precision=HIGHEST, preferred_element_type=jnp.float32
        )
        eliminate_matrix = jnp.where(
            eliminate_active_rows[:, None] & eliminate_active_cols[None, :],
            eliminate_matrix - product,
            eliminate_matrix,
        )
        eliminate_col_owner, eliminate_row_owner, eliminate_col_offset, eliminate_row_offset = (
            strip_bounds(step_index)
        )
        present = lax.dynamic_slice_in_dim(eliminate_matrix, eliminate_col_offset, PANEL, 1)
        fresh_col = jnp.where(
            (col_id == eliminate_col_owner) & eliminate_active_rows[:, None], left_strip, present
        )
        matrix = lax.dynamic_update_slice_in_dim(
            eliminate_matrix, fresh_col, eliminate_col_offset, 1
        )
        if step_index + 1 < PANELS:
            left_strip, top_strip = (left_next, top_next)
    return matrix[None]


def solution(mesh):
    placed = (
        P("front", None, "row", "column"),
        P("front", None, None),
        P("front", None, None),
        P("front", None),
        P("front", None),
        P("front", None),
        P("front", None, None, None),
    )
    return jax.shard_map(
        body, mesh=mesh, in_specs=placed, out_specs=P("front", "row", "column"), check_vma=False
    )
```

```python
import jax
import jax.numpy as jnp
from jax import lax
from jax.sharding import PartitionSpec as P

ORDER = 6144
TILE = 128
PANEL = 256
PANELS = 4
ROWMOST = 2


HIGHEST = lax.Precision.HIGHEST


def broadcast(block, axis, source):
    block = jnp.where(lax.axis_index(axis) == source, block, jnp.zeros_like(block))
    return lax.psum(block, axis)


def exchange_broadcast(block, axis, source):
    size = lax.axis_size(axis)
    if size & (size - 1):
        return broadcast(block, axis, source)
    index = lax.axis_index(axis)
    distance = 1
    while distance < size:
        partner = [(i, i ^ distance) for i in range(size)]
        received = lax.ppermute(block, axis, partner)
        take = (source // distance) % 2 != (index // distance) % 2
        block = jnp.where(take, received, block)
        distance *= 2
    return block


def pack_tiles(tile_stack, target_dev, target_spot, dest_count, capacity, sentinel):
    dest_iota = jnp.arange(dest_count, dtype=jnp.int32)
    matches = (target_dev[:, None] == dest_iota[None, :]).astype(jnp.int32)
    earlier = jnp.cumsum(matches, axis=0) - matches
    position = jnp.sum(earlier * matches, axis=1)
    usable = target_dev < dest_count
    slot_index = jnp.where(usable, target_dev * capacity + position, dest_count * capacity)
    payload = jnp.zeros((dest_count * capacity,) + tile_stack.shape[1:], tile_stack.dtype)
    payload = payload.at[slot_index].set(tile_stack, mode="drop")
    labels = (
        jnp.full((dest_count * capacity,), sentinel, jnp.int32)
        .at[slot_index]
        .set(target_spot, mode="drop")
    )
    return (
        payload.reshape((dest_count, capacity) + tile_stack.shape[1:]),
        labels.reshape(dest_count, capacity),
    )


def scatter_tiles(payload, labels, row_tiles, col_tiles):
    tile_side = payload.shape[-1]
    tile_grid = jnp.zeros((row_tiles * col_tiles + 1, tile_side, tile_side), jnp.float32)
    tile_grid = tile_grid.at[labels.reshape(-1)].add(payload.reshape(-1, tile_side, tile_side))
    tile_grid = tile_grid[: row_tiles * col_tiles]
    tile_grid = tile_grid.reshape(row_tiles, col_tiles, tile_side, tile_side).transpose(0, 2, 1, 3)
    return tile_grid.reshape(row_tiles * tile_side, col_tiles * tile_side)


def body(cbs, row_map, col_map, child_size, front_diag, panel_order, pivot_inverse):
    groups = lax.axis_size("front")
    row_devs = lax.axis_size("row")
    col_devs = lax.axis_size("column")
    row_id = lax.axis_index("row")
    col_id = lax.axis_index("column")
    children = cbs.shape[1]
    piece_rows = cbs.shape[2] // TILE
    piece_cols = cbs.shape[3] // TILE
    local_rows = ORDER // row_devs
    local_cols = ORDER // col_devs
    row_tiles = local_rows // TILE
    col_tiles = local_cols // TILE
    sentinel = row_tiles * col_tiles
    tile_stack = (
        cbs[0].reshape(children, piece_rows, TILE, piece_cols, TILE).transpose(0, 1, 3, 2, 4)
    )
    tile_stack = tile_stack.reshape(-1, TILE, TILE)
    child_rows = row_id * piece_rows + jnp.arange(piece_rows, dtype=jnp.int32)
    child_cols = col_id * piece_cols + jnp.arange(piece_cols, dtype=jnp.int32)
    parent_rows = lax.dynamic_slice_in_dim(row_map[0], row_id * piece_rows, piece_rows, 1)
    parent_cols = lax.dynamic_slice_in_dim(col_map[0], col_id * piece_cols, piece_cols, 1)
    live_rows = child_rows[None, :] < child_size[0][:, None]
    live_cols = child_cols[None, :] < child_size[0][:, None]
    owner_rows = parent_rows // row_tiles
    owner_cols = parent_cols // col_tiles
    target_spot = (
        (parent_rows - owner_rows * row_tiles)[:, :, None] * col_tiles
        + (parent_cols - owner_cols * col_tiles)[:, None, :]
    ).reshape(-1)
    usable = (live_rows[:, :, None] & live_cols[:, None, :]).reshape(-1)
    inner_dest = (owner_cols[:, None, :] * row_devs + owner_rows[:, :, None]).reshape(-1)
    all_devices = groups * row_devs * col_devs
    front_ids = jnp.arange(children, dtype=jnp.int32)[:, None]
    whole_dest = (front_ids * (row_devs * col_devs) + inner_dest.reshape(children, -1)).reshape(-1)
    whole_target = jnp.where(usable, whole_dest, all_devices)
    payload, labels = pack_tiles(
        tile_stack, whole_target, target_spot, all_devices, ROWMOST, sentinel
    )
    arrived, arrived_labels = (
        lax.all_to_all(
            payload, ("front", "column", "row"), split_axis=0, concat_axis=0, tiled=True
        ),
        lax.all_to_all(labels, ("front", "column", "row"), split_axis=0, concat_axis=0, tiled=True),
    )
    matrix = scatter_tiles(arrived, arrived_labels, row_tiles, col_tiles)
    row_glob = row_id * local_rows + jnp.arange(local_rows, dtype=jnp.int32)
    col_glob = col_id * local_cols + jnp.arange(local_cols, dtype=jnp.int32)
    diag_part = lax.dynamic_slice_in_dim(front_diag[0], row_id * local_rows, local_rows)
    matrix = matrix + jnp.where(row_glob[:, None] == col_glob[None, :], diag_part[:, None], 0.0)
    order_row = panel_order[0]
    inverses = pivot_inverse[0]
    panel_rows = local_rows // PANEL
    panel_cols = local_cols // PANEL
    row_block = row_glob // PANEL
    col_block = col_glob // PANEL

    def strip_bounds(step_index):
        pivot_block = order_row[step_index]
        return (
            pivot_block // panel_cols,
            pivot_block // panel_rows,
            pivot_block % panel_cols * PANEL,
            pivot_block % panel_rows * PANEL,
        )

    def actives(step_index):
        chosen = order_row[: step_index + 1]
        active_rows = jnp.all(row_block[:, None] != chosen[None, :], axis=1)
        active_cols = jnp.all(col_block[:, None] != chosen[None, :], axis=1)
        return (active_rows, active_cols)

    def current_strips(matrix, step_index):
        col_owner, row_owner, col_offset, row_offset = strip_bounds(step_index)
        return (
            lax.dynamic_slice_in_dim(matrix, col_offset, PANEL, 1),
            lax.dynamic_slice_in_dim(matrix, row_offset, PANEL, 0),
        )

    def share_strips(col_strip, row_strip, step_index):
        col_owner, row_owner, col_offset, row_offset = strip_bounds(step_index)
        owner_left = jnp.dot(
            col_strip, inverses[step_index], precision=HIGHEST, preferred_element_type=jnp.float32
        )
        left_strip = exchange_broadcast(owner_left, "column", col_owner)
        top_strip = exchange_broadcast(row_strip, "row", row_owner)
        return (left_strip, top_strip)

    first_col, first_row = current_strips(matrix, 0)
    left_strip, top_strip = share_strips(first_col, first_row, 0)
    for step_index in range(PANELS):
        if step_index + 1 < PANELS:
            active_rows, active_cols = actives(step_index)
            next_col, next_row = current_strips(matrix, step_index + 1)
            col_owner, row_owner, col_offset, row_offset = strip_bounds(step_index + 1)
            top_part = lax.dynamic_slice_in_dim(top_strip, col_offset, PANEL, 1)
            left_part = lax.dynamic_slice_in_dim(left_strip, row_offset, PANEL, 0)
            next_col = jnp.where(
                active_rows[:, None],
                next_col
                - jnp.dot(
                    left_strip, top_part, precision=HIGHEST, preferred_element_type=jnp.float32
                ),
                next_col,
            )
            next_row = jnp.where(
                active_cols[None, :],
                next_row
                - jnp.dot(
                    left_part, top_strip, precision=HIGHEST, preferred_element_type=jnp.float32
                ),
                next_row,
            )
            left_next, top_next = share_strips(next_col, next_row, step_index + 1)
        eliminate_matrix = matrix
        eliminate_active_rows, eliminate_active_cols = actives(step_index)
        product = jnp.dot(
            left_strip, top_strip, precision=HIGHEST, preferred_element_type=jnp.float32
        )
        eliminate_matrix = jnp.where(
            eliminate_active_rows[:, None] & eliminate_active_cols[None, :],
            eliminate_matrix - product,
            eliminate_matrix,
        )
        eliminate_col_owner, eliminate_row_owner, eliminate_col_offset, eliminate_row_offset = (
            strip_bounds(step_index)
        )
        present = lax.dynamic_slice_in_dim(eliminate_matrix, eliminate_col_offset, PANEL, 1)
        fresh_col = jnp.where(
            (col_id == eliminate_col_owner) & eliminate_active_rows[:, None], left_strip, present
        )
        matrix = lax.dynamic_update_slice_in_dim(
            eliminate_matrix, fresh_col, eliminate_col_offset, 1
        )
        if step_index + 1 < PANELS:
            left_strip, top_strip = (left_next, top_next)
    return matrix[None]


def solution(mesh):
    placed = (
        P("front", None, "row", "column"),
        P("front", None, None),
        P("front", None, None),
        P("front", None),
        P("front", None),
        P("front", None),
        P("front", None, None, None),
    )
    return jax.shard_map(
        body, mesh=mesh, in_specs=placed, out_specs=P("front", "row", "column"), check_vma=False
    )
```

```python
import jax
import jax.numpy as jnp
from jax import lax
from jax.sharding import PartitionSpec as P

ORDER = 6144
TILE = 128
PANEL = 256
PANELS = 4
ROWMOST = 2


HIGHEST = lax.Precision.HIGHEST


def broadcast(block, axis, source):
    block = jnp.where(lax.axis_index(axis) == source, block, jnp.zeros_like(block))
    return lax.psum(block, axis)


def exchange_broadcast(block, axis, source):
    size = lax.axis_size(axis)
    if size & (size - 1):
        return broadcast(block, axis, source)
    index = lax.axis_index(axis)
    distance = 1
    while distance < size:
        partner = [(i, i ^ distance) for i in range(size)]
        received = lax.ppermute(block, axis, partner)
        take = (source // distance) % 2 != (index // distance) % 2
        block = jnp.where(take, received, block)
        distance *= 2
    return block


def pack_tiles(tile_stack, target_dev, target_spot, dest_count, capacity, sentinel):
    dest_iota = jnp.arange(dest_count, dtype=jnp.int32)
    matches = (target_dev[:, None] == dest_iota[None, :]).astype(jnp.int32)
    earlier = jnp.cumsum(matches, axis=0) - matches
    position = jnp.sum(earlier * matches, axis=1)
    usable = target_dev < dest_count
    slot_index = jnp.where(usable, target_dev * capacity + position, dest_count * capacity)
    payload = jnp.zeros((dest_count * capacity,) + tile_stack.shape[1:], tile_stack.dtype)
    payload = payload.at[slot_index].set(tile_stack, mode="drop")
    labels = (
        jnp.full((dest_count * capacity,), sentinel, jnp.int32)
        .at[slot_index]
        .set(target_spot, mode="drop")
    )
    return (
        payload.reshape((dest_count, capacity) + tile_stack.shape[1:]),
        labels.reshape(dest_count, capacity),
    )


def scatter_tiles(payload, labels, row_tiles, col_tiles):
    tile_side = payload.shape[-1]
    tile_grid = jnp.zeros((row_tiles * col_tiles + 1, tile_side, tile_side), jnp.float32)
    tile_grid = tile_grid.at[labels.reshape(-1)].add(payload.reshape(-1, tile_side, tile_side))
    tile_grid = tile_grid[: row_tiles * col_tiles]
    tile_grid = tile_grid.reshape(row_tiles, col_tiles, tile_side, tile_side).transpose(0, 2, 1, 3)
    return tile_grid.reshape(row_tiles * tile_side, col_tiles * tile_side)


def body(cbs, row_map, col_map, child_size, front_diag, panel_order, pivot_inverse):
    groups = lax.axis_size("front")
    row_devs = lax.axis_size("row")
    col_devs = lax.axis_size("column")
    row_id = lax.axis_index("row")
    col_id = lax.axis_index("column")
    children = cbs.shape[1]
    piece_rows = cbs.shape[2] // TILE
    piece_cols = cbs.shape[3] // TILE
    local_rows = ORDER // row_devs
    local_cols = ORDER // col_devs
    row_tiles = local_rows // TILE
    col_tiles = local_cols // TILE
    sentinel = row_tiles * col_tiles
    tile_stack = (
        cbs[0].reshape(children, piece_rows, TILE, piece_cols, TILE).transpose(0, 1, 3, 2, 4)
    )
    tile_stack = tile_stack.reshape(-1, TILE, TILE)
    child_rows = row_id * piece_rows + jnp.arange(piece_rows, dtype=jnp.int32)
    child_cols = col_id * piece_cols + jnp.arange(piece_cols, dtype=jnp.int32)
    parent_rows = lax.dynamic_slice_in_dim(row_map[0], row_id * piece_rows, piece_rows, 1)
    parent_cols = lax.dynamic_slice_in_dim(col_map[0], col_id * piece_cols, piece_cols, 1)
    live_rows = child_rows[None, :] < child_size[0][:, None]
    live_cols = child_cols[None, :] < child_size[0][:, None]
    owner_rows = parent_rows // row_tiles
    owner_cols = parent_cols // col_tiles
    target_spot = (
        (parent_rows - owner_rows * row_tiles)[:, :, None] * col_tiles
        + (parent_cols - owner_cols * col_tiles)[:, None, :]
    ).reshape(-1)
    usable = (live_rows[:, :, None] & live_cols[:, None, :]).reshape(-1)
    inner_dest = (owner_cols[:, None, :] * row_devs + owner_rows[:, :, None]).reshape(-1)
    all_devices = groups * row_devs * col_devs
    front_ids = jnp.arange(children, dtype=jnp.int32)[:, None]
    whole_dest = (front_ids * (row_devs * col_devs) + inner_dest.reshape(children, -1)).reshape(-1)
    whole_target = jnp.where(usable, whole_dest, all_devices)
    payload, labels = pack_tiles(
        tile_stack, whole_target, target_spot, all_devices, ROWMOST, sentinel
    )
    arrived, arrived_labels = (
        lax.all_to_all(
            payload, ("front", "column", "row"), split_axis=0, concat_axis=0, tiled=True
        ),
        lax.all_to_all(labels, ("front", "column", "row"), split_axis=0, concat_axis=0, tiled=True),
    )
    matrix = scatter_tiles(arrived, arrived_labels, row_tiles, col_tiles)
    row_glob = row_id * local_rows + jnp.arange(local_rows, dtype=jnp.int32)
    col_glob = col_id * local_cols + jnp.arange(local_cols, dtype=jnp.int32)
    diag_part = lax.dynamic_slice_in_dim(front_diag[0], row_id * local_rows, local_rows)
    matrix = matrix + jnp.where(row_glob[:, None] == col_glob[None, :], diag_part[:, None], 0.0)
    order_row = panel_order[0]
    inverses = pivot_inverse[0]
    panel_rows = local_rows // PANEL
    panel_cols = local_cols // PANEL
    row_block = row_glob // PANEL
    col_block = col_glob // PANEL

    def strip_bounds(step_index):
        pivot_block = order_row[step_index]
        return (
            pivot_block // panel_cols,
            pivot_block // panel_rows,
            pivot_block % panel_cols * PANEL,
            pivot_block % panel_rows * PANEL,
        )

    def actives(step_index):
        chosen = order_row[: step_index + 1]
        active_rows = jnp.all(row_block[:, None] != chosen[None, :], axis=1)
        active_cols = jnp.all(col_block[:, None] != chosen[None, :], axis=1)
        return (active_rows, active_cols)

    def current_strips(matrix, step_index):
        col_owner, row_owner, col_offset, row_offset = strip_bounds(step_index)
        return (
            lax.dynamic_slice_in_dim(matrix, col_offset, PANEL, 1),
            lax.dynamic_slice_in_dim(matrix, row_offset, PANEL, 0),
        )

    def share_strips(col_strip, row_strip, step_index):
        col_owner, row_owner, col_offset, row_offset = strip_bounds(step_index)
        owner_left = jnp.dot(
            col_strip, inverses[step_index], precision=HIGHEST, preferred_element_type=jnp.float32
        )
        left_strip = exchange_broadcast(owner_left, "column", col_owner)
        half_cols = row_strip.shape[1] // 2
        top_strip = jnp.concatenate(
            [
                broadcast(row_strip[:, :half_cols], "row", row_owner),
                exchange_broadcast(row_strip[:, half_cols:], "row", row_owner),
            ],
            axis=1,
        )
        return (left_strip, top_strip)

    first_col, first_row = current_strips(matrix, 0)
    left_strip, top_strip = share_strips(first_col, first_row, 0)
    for step_index in range(PANELS):
        if step_index + 1 < PANELS:
            active_rows, active_cols = actives(step_index)
            next_col, next_row = current_strips(matrix, step_index + 1)
            col_owner, row_owner, col_offset, row_offset = strip_bounds(step_index + 1)
            top_part = lax.dynamic_slice_in_dim(top_strip, col_offset, PANEL, 1)
            left_part = lax.dynamic_slice_in_dim(left_strip, row_offset, PANEL, 0)
            next_col = jnp.where(
                active_rows[:, None],
                next_col
                - jnp.dot(
                    left_strip, top_part, precision=HIGHEST, preferred_element_type=jnp.float32
                ),
                next_col,
            )
            next_row = jnp.where(
                active_cols[None, :],
                next_row
                - jnp.dot(
                    left_part, top_strip, precision=HIGHEST, preferred_element_type=jnp.float32
                ),
                next_row,
            )
            left_next, top_next = share_strips(next_col, next_row, step_index + 1)
        eliminate_matrix = matrix
        eliminate_active_rows, eliminate_active_cols = actives(step_index)
        product = jnp.dot(
            left_strip, top_strip, precision=HIGHEST, preferred_element_type=jnp.float32
        )
        eliminate_matrix = jnp.where(
            eliminate_active_rows[:, None] & eliminate_active_cols[None, :],
            eliminate_matrix - product,
            eliminate_matrix,
        )
        eliminate_col_owner, eliminate_row_owner, eliminate_col_offset, eliminate_row_offset = (
            strip_bounds(step_index)
        )
        present = lax.dynamic_slice_in_dim(eliminate_matrix, eliminate_col_offset, PANEL, 1)
        fresh_col = jnp.where(
            (col_id == eliminate_col_owner) & eliminate_active_rows[:, None], left_strip, present
        )
        matrix = lax.dynamic_update_slice_in_dim(
            eliminate_matrix, fresh_col, eliminate_col_offset, 1
        )
        if step_index + 1 < PANELS:
            left_strip, top_strip = (left_next, top_next)
    return matrix[None]


def solution(mesh):
    placed = (
        P("front", None, "row", "column"),
        P("front", None, None),
        P("front", None, None),
        P("front", None),
        P("front", None),
        P("front", None),
        P("front", None, None, None),
    )
    return jax.shard_map(
        body, mesh=mesh, in_specs=placed, out_specs=P("front", "row", "column"), check_vma=False
    )
```

```python
import jax
import jax.numpy as jnp
from jax import lax
from jax.sharding import PartitionSpec as P

ORDER = 6144
TILE = 128
PANEL = 256
PANELS = 4
ROWMOST = 2


HIGHEST = lax.Precision.HIGHEST


def broadcast(block, axis, source):
    block = jnp.where(lax.axis_index(axis) == source, block, jnp.zeros_like(block))
    return lax.psum(block, axis)


def exchange_broadcast(block, axis, source):
    size = lax.axis_size(axis)
    if size & (size - 1):
        return broadcast(block, axis, source)
    index = lax.axis_index(axis)
    distance = 1
    while distance < size:
        partner = [(i, i ^ distance) for i in range(size)]
        received = lax.ppermute(block, axis, partner)
        take = (source // distance) % 2 != (index // distance) % 2
        block = jnp.where(take, received, block)
        distance *= 2
    return block


def pack_tiles(tile_stack, target_dev, target_spot, dest_count, capacity, sentinel):
    dest_iota = jnp.arange(dest_count, dtype=jnp.int32)
    matches = (target_dev[:, None] == dest_iota[None, :]).astype(jnp.int32)
    earlier = jnp.cumsum(matches, axis=0) - matches
    position = jnp.sum(earlier * matches, axis=1)
    usable = target_dev < dest_count
    slot_index = jnp.where(usable, target_dev * capacity + position, dest_count * capacity)
    payload = jnp.zeros((dest_count * capacity,) + tile_stack.shape[1:], tile_stack.dtype)
    payload = payload.at[slot_index].set(tile_stack, mode="drop")
    labels = (
        jnp.full((dest_count * capacity,), sentinel, jnp.int32)
        .at[slot_index]
        .set(target_spot, mode="drop")
    )
    return (
        payload.reshape((dest_count, capacity) + tile_stack.shape[1:]),
        labels.reshape(dest_count, capacity),
    )


def scatter_tiles(payload, labels, base, row_tiles, col_tiles):
    tile_side = payload.shape[-1]
    spots = labels.reshape(-1)
    tile_rows = spots // col_tiles
    tile_cols = spots % col_tiles
    grid = base.reshape(row_tiles, tile_side, col_tiles, tile_side)
    grid = grid.at[tile_rows, :, tile_cols, :].add(
        payload.reshape(-1, tile_side, tile_side), mode="drop"
    )
    return grid.reshape(row_tiles * tile_side, col_tiles * tile_side)


def body(cbs, row_map, col_map, child_size, front_diag, panel_order, pivot_inverse):
    groups = lax.axis_size("front")
    row_devs = lax.axis_size("row")
    col_devs = lax.axis_size("column")
    row_id = lax.axis_index("row")
    col_id = lax.axis_index("column")
    children = cbs.shape[1]
    piece_rows = cbs.shape[2] // TILE
    piece_cols = cbs.shape[3] // TILE
    local_rows = ORDER // row_devs
    local_cols = ORDER // col_devs
    row_tiles = local_rows // TILE
    col_tiles = local_cols // TILE
    sentinel = row_tiles * col_tiles
    tile_stack = (
        cbs[0].reshape(children, piece_rows, TILE, piece_cols, TILE).transpose(0, 1, 3, 2, 4)
    )
    tile_stack = tile_stack.reshape(-1, TILE, TILE)
    child_rows = row_id * piece_rows + jnp.arange(piece_rows, dtype=jnp.int32)
    child_cols = col_id * piece_cols + jnp.arange(piece_cols, dtype=jnp.int32)
    parent_rows = lax.dynamic_slice_in_dim(row_map[0], row_id * piece_rows, piece_rows, 1)
    parent_cols = lax.dynamic_slice_in_dim(col_map[0], col_id * piece_cols, piece_cols, 1)
    live_rows = child_rows[None, :] < child_size[0][:, None]
    live_cols = child_cols[None, :] < child_size[0][:, None]
    owner_rows = parent_rows // row_tiles
    owner_cols = parent_cols // col_tiles
    target_spot = (
        (parent_rows - owner_rows * row_tiles)[:, :, None] * col_tiles
        + (parent_cols - owner_cols * col_tiles)[:, None, :]
    ).reshape(-1)
    usable = (live_rows[:, :, None] & live_cols[:, None, :]).reshape(-1)
    inner_dest = (owner_cols[:, None, :] * row_devs + owner_rows[:, :, None]).reshape(-1)
    all_devices = groups * row_devs * col_devs
    front_ids = jnp.arange(children, dtype=jnp.int32)[:, None]
    whole_dest = (front_ids * (row_devs * col_devs) + inner_dest.reshape(children, -1)).reshape(-1)
    whole_target = jnp.where(usable, whole_dest, all_devices)
    payload, labels = pack_tiles(
        tile_stack, whole_target, target_spot, all_devices, ROWMOST, sentinel
    )
    arrived, arrived_labels = (
        lax.all_to_all(
            payload, ("front", "column", "row"), split_axis=0, concat_axis=0, tiled=True
        ),
        lax.all_to_all(labels, ("front", "column", "row"), split_axis=0, concat_axis=0, tiled=True),
    )
    row_glob = row_id * local_rows + jnp.arange(local_rows, dtype=jnp.int32)
    col_glob = col_id * local_cols + jnp.arange(local_cols, dtype=jnp.int32)
    diag_part = lax.dynamic_slice_in_dim(front_diag[0], row_id * local_rows, local_rows)
    diag_block = jnp.where(row_glob[:, None] == col_glob[None, :], diag_part[:, None], 0.0)
    matrix = scatter_tiles(arrived, arrived_labels, diag_block, row_tiles, col_tiles)
    order_row = panel_order[0]
    inverses = pivot_inverse[0]
    panel_rows = local_rows // PANEL
    panel_cols = local_cols // PANEL
    row_block = row_glob // PANEL
    col_block = col_glob // PANEL

    def strip_bounds(step_index):
        pivot_block = order_row[step_index]
        return (
            pivot_block // panel_cols,
            pivot_block // panel_rows,
            pivot_block % panel_cols * PANEL,
            pivot_block % panel_rows * PANEL,
        )

    def actives(step_index):
        chosen = order_row[: step_index + 1]
        active_rows = jnp.all(row_block[:, None] != chosen[None, :], axis=1)
        active_cols = jnp.all(col_block[:, None] != chosen[None, :], axis=1)
        return (active_rows, active_cols)

    def current_strips(matrix, step_index):
        col_owner, row_owner, col_offset, row_offset = strip_bounds(step_index)
        return (
            lax.dynamic_slice_in_dim(matrix, col_offset, PANEL, 1),
            lax.dynamic_slice_in_dim(matrix, row_offset, PANEL, 0),
        )

    def share_strips(col_strip, row_strip, step_index):
        col_owner, row_owner, col_offset, row_offset = strip_bounds(step_index)
        owner_left = jnp.dot(
            col_strip, inverses[step_index], precision=HIGHEST, preferred_element_type=jnp.float32
        )
        left_strip = exchange_broadcast(owner_left, "column", col_owner)
        top_strip = broadcast(row_strip, "row", row_owner)
        return (left_strip, top_strip)

    first_col, first_row = current_strips(matrix, 0)
    left_strip, top_strip = share_strips(first_col, first_row, 0)
    for step_index in range(PANELS):
        if step_index + 1 < PANELS:
            active_rows, active_cols = actives(step_index)
            next_col, next_row = current_strips(matrix, step_index + 1)
            col_owner, row_owner, col_offset, row_offset = strip_bounds(step_index + 1)
            top_part = lax.dynamic_slice_in_dim(top_strip, col_offset, PANEL, 1)
            left_part = lax.dynamic_slice_in_dim(left_strip, row_offset, PANEL, 0)
            next_col = jnp.where(
                active_rows[:, None],
                next_col
                - jnp.dot(
                    left_strip, top_part, precision=HIGHEST, preferred_element_type=jnp.float32
                ),
                next_col,
            )
            next_row = jnp.where(
                active_cols[None, :],
                next_row
                - jnp.dot(
                    left_part, top_strip, precision=HIGHEST, preferred_element_type=jnp.float32
                ),
                next_row,
            )
            left_next, top_next = share_strips(next_col, next_row, step_index + 1)
        eliminate_matrix = matrix
        eliminate_active_rows, eliminate_active_cols = actives(step_index)
        product = jnp.dot(
            left_strip, top_strip, precision=HIGHEST, preferred_element_type=jnp.float32
        )
        eliminate_matrix = jnp.where(
            eliminate_active_rows[:, None] & eliminate_active_cols[None, :],
            eliminate_matrix - product,
            eliminate_matrix,
        )
        eliminate_col_owner, eliminate_row_owner, eliminate_col_offset, eliminate_row_offset = (
            strip_bounds(step_index)
        )
        present = lax.dynamic_slice_in_dim(eliminate_matrix, eliminate_col_offset, PANEL, 1)
        fresh_col = jnp.where(
            (col_id == eliminate_col_owner) & eliminate_active_rows[:, None], left_strip, present
        )
        matrix = lax.dynamic_update_slice_in_dim(
            eliminate_matrix, fresh_col, eliminate_col_offset, 1
        )
        if step_index + 1 < PANELS:
            left_strip, top_strip = (left_next, top_next)
    return matrix[None]


def solution(mesh):
    placed = (
        P("front", None, "row", "column"),
        P("front", None, None),
        P("front", None, None),
        P("front", None),
        P("front", None),
        P("front", None),
        P("front", None, None, None),
    )
    return jax.shard_map(
        body, mesh=mesh, in_specs=placed, out_specs=P("front", "row", "column"), check_vma=False
    )
```

```python
import jax
import jax.numpy as jnp
from jax import lax
from jax.sharding import PartitionSpec as P

ORDER = 6144
TILE = 128
PANEL = 256
PANELS = 4
ROWMOST = 2


HIGHEST = lax.Precision.HIGHEST


def broadcast(block, axis, source):
    block = jnp.where(lax.axis_index(axis) == source, block, jnp.zeros_like(block))
    return lax.psum(block, axis)


def exchange_broadcast(block, axis, source):
    size = lax.axis_size(axis)
    if size & (size - 1):
        return broadcast(block, axis, source)
    index = lax.axis_index(axis)
    distance = 1
    while distance < size:
        partner = [(i, i ^ distance) for i in range(size)]
        received = lax.ppermute(block, axis, partner)
        take = (source // distance) % 2 != (index // distance) % 2
        block = jnp.where(take, received, block)
        distance *= 2
    return block


def pack_tiles(tile_stack, target_dev, target_spot, dest_count, capacity, sentinel):
    dest_iota = jnp.arange(dest_count, dtype=jnp.int32)
    matches = (target_dev[:, None] == dest_iota[None, :]).astype(jnp.int32)
    earlier = jnp.cumsum(matches, axis=0) - matches
    position = jnp.sum(earlier * matches, axis=1)
    usable = target_dev < dest_count
    slot_index = jnp.where(usable, target_dev * capacity + position, dest_count * capacity)
    payload = jnp.zeros((dest_count * capacity,) + tile_stack.shape[1:], tile_stack.dtype)
    payload = payload.at[slot_index].set(tile_stack, mode="drop")
    labels = (
        jnp.full((dest_count * capacity,), sentinel, jnp.int32)
        .at[slot_index]
        .set(target_spot, mode="drop")
    )
    return (
        payload.reshape((dest_count, capacity) + tile_stack.shape[1:]),
        labels.reshape(dest_count, capacity),
    )


def scatter_tiles(payload, labels, base, row_tiles, col_tiles):
    tile_side = payload.shape[-1]
    spots = labels.reshape(-1)
    tile_rows = spots // col_tiles
    tile_cols = spots % col_tiles
    grid = base.reshape(row_tiles, tile_side, col_tiles, tile_side)
    grid = grid.at[tile_rows, :, tile_cols, :].add(
        payload.reshape(-1, tile_side, tile_side), mode="drop"
    )
    return grid.reshape(row_tiles * tile_side, col_tiles * tile_side)


def body(cbs, row_map, col_map, child_size, front_diag, panel_order, pivot_inverse):
    groups = lax.axis_size("front")
    row_devs = lax.axis_size("row")
    col_devs = lax.axis_size("column")
    row_id = lax.axis_index("row")
    col_id = lax.axis_index("column")
    children = cbs.shape[1]
    piece_rows = cbs.shape[2] // TILE
    piece_cols = cbs.shape[3] // TILE
    local_rows = ORDER // row_devs
    local_cols = ORDER // col_devs
    row_tiles = local_rows // TILE
    col_tiles = local_cols // TILE
    sentinel = row_tiles * col_tiles
    tile_stack = (
        cbs[0].reshape(children, piece_rows, TILE, piece_cols, TILE).transpose(0, 1, 3, 2, 4)
    )
    tile_stack = tile_stack.reshape(-1, TILE, TILE)
    child_rows = row_id * piece_rows + jnp.arange(piece_rows, dtype=jnp.int32)
    child_cols = col_id * piece_cols + jnp.arange(piece_cols, dtype=jnp.int32)
    parent_rows = lax.dynamic_slice_in_dim(row_map[0], row_id * piece_rows, piece_rows, 1)
    parent_cols = lax.dynamic_slice_in_dim(col_map[0], col_id * piece_cols, piece_cols, 1)
    live_rows = child_rows[None, :] < child_size[0][:, None]
    live_cols = child_cols[None, :] < child_size[0][:, None]
    owner_rows = parent_rows // row_tiles
    owner_cols = parent_cols // col_tiles
    target_spot = (
        (parent_rows - owner_rows * row_tiles)[:, :, None] * col_tiles
        + (parent_cols - owner_cols * col_tiles)[:, None, :]
    ).reshape(-1)
    usable = (live_rows[:, :, None] & live_cols[:, None, :]).reshape(-1)
    inner_dest = (owner_cols[:, None, :] * row_devs + owner_rows[:, :, None]).reshape(-1)
    all_devices = groups * row_devs * col_devs
    front_ids = jnp.arange(children, dtype=jnp.int32)[:, None]
    whole_dest = (front_ids * (row_devs * col_devs) + inner_dest.reshape(children, -1)).reshape(-1)
    whole_target = jnp.where(usable, whole_dest, all_devices)
    payload, labels = pack_tiles(
        tile_stack, whole_target, target_spot, all_devices, ROWMOST, sentinel
    )
    arrived, arrived_labels = (
        lax.all_to_all(
            payload, ("front", "column", "row"), split_axis=0, concat_axis=0, tiled=True
        ),
        lax.all_to_all(labels, ("front", "column", "row"), split_axis=0, concat_axis=0, tiled=True),
    )
    row_glob = row_id * local_rows + jnp.arange(local_rows, dtype=jnp.int32)
    col_glob = col_id * local_cols + jnp.arange(local_cols, dtype=jnp.int32)
    diag_part = lax.dynamic_slice_in_dim(front_diag[0], row_id * local_rows, local_rows)
    diag_block = jnp.where(row_glob[:, None] == col_glob[None, :], diag_part[:, None], 0.0)
    matrix = scatter_tiles(arrived, arrived_labels, diag_block, row_tiles, col_tiles)
    order_row = panel_order[0]
    inverses = pivot_inverse[0]
    panel_rows = local_rows // PANEL
    panel_cols = local_cols // PANEL
    row_block = row_glob // PANEL
    col_block = col_glob // PANEL

    def strip_bounds(step_index):
        pivot_block = order_row[step_index]
        return (
            pivot_block // panel_cols,
            pivot_block // panel_rows,
            pivot_block % panel_cols * PANEL,
            pivot_block % panel_rows * PANEL,
        )

    def actives(step_index):
        chosen = order_row[: step_index + 1]
        active_rows = jnp.all(row_block[:, None] != chosen[None, :], axis=1)
        active_cols = jnp.all(col_block[:, None] != chosen[None, :], axis=1)
        return (active_rows, active_cols)

    def current_strips(matrix, step_index):
        col_owner, row_owner, col_offset, row_offset = strip_bounds(step_index)
        return (
            lax.dynamic_slice_in_dim(matrix, col_offset, PANEL, 1),
            lax.dynamic_slice_in_dim(matrix, row_offset, PANEL, 0),
        )

    def share_strips(col_strip, row_strip, step_index):
        col_owner, row_owner, col_offset, row_offset = strip_bounds(step_index)
        owner_left = jnp.dot(
            col_strip, inverses[step_index], precision=HIGHEST, preferred_element_type=jnp.float32
        )
        left_strip = exchange_broadcast(owner_left, "column", col_owner)
        top_strip = broadcast(row_strip, "row", row_owner)
        return (left_strip, top_strip)

    first_col, first_row = current_strips(matrix, 0)
    left_strip, top_strip = share_strips(first_col, first_row, 0)
    for step_index in range(PANELS):
        if step_index + 1 < PANELS:
            active_rows, active_cols = actives(step_index)
            next_col, next_row = current_strips(matrix, step_index + 1)
            col_owner, row_owner, col_offset, row_offset = strip_bounds(step_index + 1)
            top_part = lax.dynamic_slice_in_dim(top_strip, col_offset, PANEL, 1)
            left_part = lax.dynamic_slice_in_dim(left_strip, row_offset, PANEL, 0)
            next_row = jnp.where(
                active_cols[None, :],
                next_row
                - jnp.dot(
                    left_part, top_strip, precision=HIGHEST, preferred_element_type=jnp.float32
                ),
                next_row,
            )
            next_row, next_col = lax.optimization_barrier((next_row, next_col))
            next_col = jnp.where(
                active_rows[:, None],
                next_col
                - jnp.dot(
                    left_strip, top_part, precision=HIGHEST, preferred_element_type=jnp.float32
                ),
                next_col,
            )
            left_next, top_next = share_strips(next_col, next_row, step_index + 1)
        eliminate_matrix = matrix
        eliminate_active_rows, eliminate_active_cols = actives(step_index)
        product = jnp.dot(
            left_strip, top_strip, precision=HIGHEST, preferred_element_type=jnp.float32
        )
        eliminate_matrix = jnp.where(
            eliminate_active_rows[:, None] & eliminate_active_cols[None, :],
            eliminate_matrix - product,
            eliminate_matrix,
        )
        eliminate_col_owner, eliminate_row_owner, eliminate_col_offset, eliminate_row_offset = (
            strip_bounds(step_index)
        )
        present = lax.dynamic_slice_in_dim(eliminate_matrix, eliminate_col_offset, PANEL, 1)
        fresh_col = jnp.where(
            (col_id == eliminate_col_owner) & eliminate_active_rows[:, None], left_strip, present
        )
        matrix = lax.dynamic_update_slice_in_dim(
            eliminate_matrix, fresh_col, eliminate_col_offset, 1
        )
        if step_index + 1 < PANELS:
            left_strip, top_strip = (left_next, top_next)
    return matrix[None]


def solution(mesh):
    placed = (
        P("front", None, "row", "column"),
        P("front", None, None),
        P("front", None, None),
        P("front", None),
        P("front", None),
        P("front", None),
        P("front", None, None, None),
    )
    return jax.shard_map(
        body, mesh=mesh, in_specs=placed, out_specs=P("front", "row", "column"), check_vma=False
    )
```

```python
import jax
import jax.numpy as jnp
from jax import lax
from jax.sharding import PartitionSpec as P

ORDER = 6144
TILE = 128
PANEL = 256
PANELS = 4
ROWMOST = 2


HIGHEST = lax.Precision.HIGHEST


def broadcast(block, axis, source):
    block = jnp.where(lax.axis_index(axis) == source, block, jnp.zeros_like(block))
    return lax.psum(block, axis)


def exchange_broadcast(block, axis, source):
    size = lax.axis_size(axis)
    if size & (size - 1):
        return broadcast(block, axis, source)
    index = lax.axis_index(axis)
    distance = 1
    while distance < size:
        partner = [(i, i ^ distance) for i in range(size)]
        received = lax.ppermute(block, axis, partner)
        take = (source // distance) % 2 != (index // distance) % 2
        block = jnp.where(take, received, block)
        distance *= 2
    return block


def pack_tiles(tile_stack, target_dev, target_spot, dest_count, capacity, sentinel):
    dest_iota = jnp.arange(dest_count, dtype=jnp.int32)
    matches = (target_dev[:, None] == dest_iota[None, :]).astype(jnp.int32)
    earlier = jnp.cumsum(matches, axis=0) - matches
    position = jnp.sum(earlier * matches, axis=1)
    usable = target_dev < dest_count
    slot_index = jnp.where(usable, target_dev * capacity + position, dest_count * capacity)
    payload = jnp.zeros((dest_count * capacity,) + tile_stack.shape[1:], tile_stack.dtype)
    payload = payload.at[slot_index].set(tile_stack, mode="drop")
    labels = (
        jnp.full((dest_count * capacity,), sentinel, jnp.int32)
        .at[slot_index]
        .set(target_spot, mode="drop")
    )
    return (
        payload.reshape((dest_count, capacity) + tile_stack.shape[1:]),
        labels.reshape(dest_count, capacity),
    )


def scatter_tiles(payload, labels, base, row_tiles, col_tiles):
    tile_side = payload.shape[-1]
    spots = labels.reshape(-1)
    tile_rows = spots // col_tiles
    tile_cols = spots % col_tiles
    grid = base.reshape(row_tiles, tile_side, col_tiles, tile_side)
    grid = grid.at[tile_rows, :, tile_cols, :].add(
        payload.reshape(-1, tile_side, tile_side), mode="drop"
    )
    return grid.reshape(row_tiles * tile_side, col_tiles * tile_side)


def arrival_labels(
    row_map, col_map, child_size, groups, row_devs, col_devs, piece_rows, piece_cols,
    row_tiles, col_tiles, sentinel,
):
    children, side = row_map.shape[1], row_map.shape[2]
    span = children * side
    maps = jnp.concatenate(
        [row_map[0].reshape(-1), col_map[0].reshape(-1), child_size[0].reshape(-1)]
    )
    every = lax.all_gather(maps, "front")
    front_id = lax.axis_index("front")
    row_maps = every[:, :span].reshape(groups, children, side)[:, front_id]
    col_maps = every[:, span : 2 * span].reshape(groups, children, side)[:, front_id]
    sizes = every[:, 2 * span :].reshape(groups, children)[:, front_id]
    child_rows = (
        jnp.arange(row_devs, dtype=jnp.int32)[:, None] * piece_rows
        + jnp.arange(piece_rows, dtype=jnp.int32)[None, :]
    )
    child_cols = (
        jnp.arange(col_devs, dtype=jnp.int32)[:, None] * piece_cols
        + jnp.arange(piece_cols, dtype=jnp.int32)[None, :]
    )
    parent_rows = row_maps[:, child_rows]
    parent_cols = col_maps[:, child_cols]
    hit_rows = (child_rows[None] < sizes[:, None, None]) & (
        parent_rows // row_tiles == lax.axis_index("row")
    )
    hit_cols = (child_cols[None] < sizes[:, None, None]) & (
        parent_cols // col_tiles == lax.axis_index("column")
    )
    hit = hit_cols[:, :, None, None, :] & hit_rows[:, None, :, :, None]
    spot = (parent_rows % row_tiles)[:, None, :, :, None] * col_tiles + (
        parent_cols % col_tiles
    )[:, :, None, None, :]
    sources = groups * col_devs * row_devs
    hit = hit.reshape(sources, piece_rows * piece_cols).astype(jnp.int32)
    spot = jnp.broadcast_to(
        spot, (groups, col_devs, row_devs, piece_rows, piece_cols)
    ).reshape(sources, piece_rows * piece_cols)
    rank = jnp.cumsum(hit, axis=1) - hit
    slots = []
    for slot in range(ROWMOST):
        chosen = (hit == 1) & (rank == slot)
        slots.append(
            jnp.where(
                jnp.any(chosen, axis=1), jnp.sum(jnp.where(chosen, spot, 0), axis=1), sentinel
            )
        )
    return jnp.stack(slots, axis=1)


def body(cbs, row_map, col_map, child_size, front_diag, panel_order, pivot_inverse):
    groups = lax.axis_size("front")
    row_devs = lax.axis_size("row")
    col_devs = lax.axis_size("column")
    row_id = lax.axis_index("row")
    col_id = lax.axis_index("column")
    children = cbs.shape[1]
    piece_rows = cbs.shape[2] // TILE
    piece_cols = cbs.shape[3] // TILE
    local_rows = ORDER // row_devs
    local_cols = ORDER // col_devs
    row_tiles = local_rows // TILE
    col_tiles = local_cols // TILE
    sentinel = row_tiles * col_tiles
    tile_stack = (
        cbs[0].reshape(children, piece_rows, TILE, piece_cols, TILE).transpose(0, 1, 3, 2, 4)
    )
    tile_stack = tile_stack.reshape(-1, TILE, TILE)
    child_rows = row_id * piece_rows + jnp.arange(piece_rows, dtype=jnp.int32)
    child_cols = col_id * piece_cols + jnp.arange(piece_cols, dtype=jnp.int32)
    parent_rows = lax.dynamic_slice_in_dim(row_map[0], row_id * piece_rows, piece_rows, 1)
    parent_cols = lax.dynamic_slice_in_dim(col_map[0], col_id * piece_cols, piece_cols, 1)
    live_rows = child_rows[None, :] < child_size[0][:, None]
    live_cols = child_cols[None, :] < child_size[0][:, None]
    owner_rows = parent_rows // row_tiles
    owner_cols = parent_cols // col_tiles
    target_spot = (
        (parent_rows - owner_rows * row_tiles)[:, :, None] * col_tiles
        + (parent_cols - owner_cols * col_tiles)[:, None, :]
    ).reshape(-1)
    usable = (live_rows[:, :, None] & live_cols[:, None, :]).reshape(-1)
    inner_dest = (owner_cols[:, None, :] * row_devs + owner_rows[:, :, None]).reshape(-1)
    all_devices = groups * row_devs * col_devs
    front_ids = jnp.arange(children, dtype=jnp.int32)[:, None]
    whole_dest = (front_ids * (row_devs * col_devs) + inner_dest.reshape(children, -1)).reshape(-1)
    whole_target = jnp.where(usable, whole_dest, all_devices)
    payload, labels = pack_tiles(
        tile_stack, whole_target, target_spot, all_devices, ROWMOST, sentinel
    )
    arrived = lax.all_to_all(
        payload, ("front", "column", "row"), split_axis=0, concat_axis=0, tiled=True
    )
    arrived_labels = arrival_labels(
        row_map, col_map, child_size, groups, row_devs, col_devs, piece_rows, piece_cols,
        row_tiles, col_tiles, sentinel,
    )
    row_glob = row_id * local_rows + jnp.arange(local_rows, dtype=jnp.int32)
    col_glob = col_id * local_cols + jnp.arange(local_cols, dtype=jnp.int32)
    diag_part = lax.dynamic_slice_in_dim(front_diag[0], row_id * local_rows, local_rows)
    diag_block = jnp.where(row_glob[:, None] == col_glob[None, :], diag_part[:, None], 0.0)
    matrix = scatter_tiles(arrived, arrived_labels, diag_block, row_tiles, col_tiles)
    order_row = panel_order[0]
    inverses = pivot_inverse[0]
    panel_rows = local_rows // PANEL
    panel_cols = local_cols // PANEL
    row_block = row_glob // PANEL
    col_block = col_glob // PANEL

    def strip_bounds(step_index):
        pivot_block = order_row[step_index]
        return (
            pivot_block // panel_cols,
            pivot_block // panel_rows,
            pivot_block % panel_cols * PANEL,
            pivot_block % panel_rows * PANEL,
        )

    def actives(step_index):
        chosen = order_row[: step_index + 1]
        active_rows = jnp.all(row_block[:, None] != chosen[None, :], axis=1)
        active_cols = jnp.all(col_block[:, None] != chosen[None, :], axis=1)
        return (active_rows, active_cols)

    def current_strips(matrix, step_index):
        col_owner, row_owner, col_offset, row_offset = strip_bounds(step_index)
        return (
            lax.dynamic_slice_in_dim(matrix, col_offset, PANEL, 1),
            lax.dynamic_slice_in_dim(matrix, row_offset, PANEL, 0),
        )

    def share_strips(col_strip, row_strip, step_index):
        col_owner, row_owner, col_offset, row_offset = strip_bounds(step_index)
        owner_left = jnp.dot(
            col_strip, inverses[step_index], precision=HIGHEST, preferred_element_type=jnp.float32
        )
        left_strip = exchange_broadcast(owner_left, "column", col_owner)
        top_strip = lax.psum(row_strip, "row")
        return (left_strip, top_strip)

    def owned_rows(row_strip, step_index):
        col_owner, row_owner, col_offset, row_offset = strip_bounds(step_index)
        return jnp.where(row_id == row_owner, row_strip, jnp.zeros_like(row_strip))

    first_col, first_row = current_strips(matrix, 0)
    left_strip, top_strip = share_strips(first_col, owned_rows(first_row, 0), 0)
    for step_index in range(PANELS):
        if step_index + 1 < PANELS:
            active_rows, active_cols = actives(step_index)
            next_col, next_row = current_strips(matrix, step_index + 1)
            col_owner, row_owner, col_offset, row_offset = strip_bounds(step_index + 1)
            top_part = lax.dynamic_slice_in_dim(top_strip, col_offset, PANEL, 1)
            left_part = lax.dynamic_slice_in_dim(left_strip, row_offset, PANEL, 0)
            next_row = jnp.where(
                active_cols[None, :],
                next_row
                - jnp.dot(
                    left_part, top_strip, precision=HIGHEST, preferred_element_type=jnp.float32
                ),
                next_row,
            )
            next_row = owned_rows(next_row, step_index + 1)
            next_row, next_col = lax.optimization_barrier((next_row, next_col))
            next_col = jnp.where(
                active_rows[:, None],
                next_col
                - jnp.dot(
                    left_strip, top_part, precision=HIGHEST, preferred_element_type=jnp.float32
                ),
                next_col,
            )
            left_next, top_next = share_strips(next_col, next_row, step_index + 1)
        eliminate_matrix = matrix
        eliminate_active_rows, eliminate_active_cols = actives(step_index)
        product = jnp.dot(
            left_strip, top_strip, precision=HIGHEST, preferred_element_type=jnp.float32
        )
        eliminate_matrix = jnp.where(
            eliminate_active_rows[:, None] & eliminate_active_cols[None, :],
            eliminate_matrix - product,
            eliminate_matrix,
        )
        eliminate_col_owner, eliminate_row_owner, eliminate_col_offset, eliminate_row_offset = (
            strip_bounds(step_index)
        )
        present = lax.dynamic_slice_in_dim(eliminate_matrix, eliminate_col_offset, PANEL, 1)
        fresh_col = jnp.where(
            (col_id == eliminate_col_owner) & eliminate_active_rows[:, None], left_strip, present
        )
        matrix = lax.dynamic_update_slice_in_dim(
            eliminate_matrix, fresh_col, eliminate_col_offset, 1
        )
        if step_index + 1 < PANELS:
            left_strip, top_strip = (left_next, top_next)
    return matrix[None]


def solution(mesh):
    placed = (
        P("front", None, "row", "column"),
        P("front", None, None),
        P("front", None, None),
        P("front", None),
        P("front", None),
        P("front", None),
        P("front", None, None, None),
    )
    return jax.shard_map(
        body, mesh=mesh, in_specs=placed, out_specs=P("front", "row", "column"), check_vma=False
    )
```

```python
import jax
import jax.numpy as jnp
from jax import lax
from jax.sharding import PartitionSpec as P
from jax.experimental import pallas as pl
from jax.experimental.pallas import tpu as pltpu

ORDER = 6144
TILE = 128
PANEL = 256
PANELS = 4
ROWMOST = 2


HIGHEST = lax.Precision.HIGHEST


def broadcast(block, axis, source):
    block = jnp.where(lax.axis_index(axis) == source, block, jnp.zeros_like(block))
    return lax.psum(block, axis)


def exchange_broadcast(block, axis, source):
    size = lax.axis_size(axis)
    if size & (size - 1):
        return broadcast(block, axis, source)
    index = lax.axis_index(axis)
    distance = 1
    while distance < size:
        partner = [(i, i ^ distance) for i in range(size)]
        received = lax.ppermute(block, axis, partner)
        take = (source // distance) % 2 != (index // distance) % 2
        block = jnp.where(take, received, block)
        distance *= 2
    return block


def pack_tiles(tile_stack, target_dev, target_spot, dest_count, capacity, sentinel):
    dest_iota = jnp.arange(dest_count, dtype=jnp.int32)
    matches = (target_dev[:, None] == dest_iota[None, :]).astype(jnp.int32)
    earlier = jnp.cumsum(matches, axis=0) - matches
    position = jnp.sum(earlier * matches, axis=1)
    usable = target_dev < dest_count
    slot_index = jnp.where(usable, target_dev * capacity + position, dest_count * capacity)
    payload = jnp.zeros((dest_count * capacity,) + tile_stack.shape[1:], tile_stack.dtype)
    payload = payload.at[slot_index].set(tile_stack, mode="drop")
    labels = (
        jnp.full((dest_count * capacity,), sentinel, jnp.int32)
        .at[slot_index]
        .set(target_spot, mode="drop")
    )
    return (
        payload.reshape((dest_count, capacity) + tile_stack.shape[1:]),
        labels.reshape(dest_count, capacity),
    )


def assemble_kernel(spots_ref, offset_ref, diag_ref, payload_ref, out_ref):
    rows_total, cols_total = out_ref.shape
    tile_side = payload_ref.shape[-1]
    row_tiles = rows_total // tile_side
    col_tiles = cols_total // tile_side
    offset = offset_ref[0]
    for band in range(row_tiles):
        band_rows = pl.ds(band * tile_side, tile_side)
        row_iota = lax.broadcasted_iota(jnp.int32, (tile_side, cols_total), 0) + band * tile_side
        col_iota = lax.broadcasted_iota(jnp.int32, (tile_side, cols_total), 1)
        out_ref[band_rows, :] = jnp.where(
            row_iota + offset == col_iota, diag_ref[band_rows, :], 0.0
        )

    def add_tile(slot, carry):
        spot = spots_ref[slot]
        tile_row = spot // col_tiles
        tile_col = spot % col_tiles

        @pl.when(tile_row < row_tiles)
        def _():
            row_start = pl.multiple_of(tile_row * tile_side, tile_side)
            col_start = pl.multiple_of(tile_col * tile_side, tile_side)
            window = (pl.ds(row_start, tile_side), pl.ds(col_start, tile_side))
            out_ref[window] = out_ref[window] + payload_ref[slot]

        return carry

    lax.fori_loop(0, payload_ref.shape[0], add_tile, 0)


def scatter_tiles(payload, labels, diag_part, offset, local_rows, local_cols):
    tile_side = payload.shape[-1]
    tiles = payload.reshape(-1, tile_side, tile_side)
    slots = tiles.shape[0]
    return pl.pallas_call(
        assemble_kernel,
        out_shape=jax.ShapeDtypeStruct((local_rows, local_cols), jnp.float32),
        grid_spec=pltpu.PrefetchScalarGridSpec(
            num_scalar_prefetch=2,
            grid=(1,),
            in_specs=[
                pl.BlockSpec((local_rows, 1), lambda i, *_: (0, 0)),
                pl.BlockSpec((slots, tile_side, tile_side), lambda i, *_: (0, 0, 0)),
            ],
            out_specs=pl.BlockSpec((local_rows, local_cols), lambda i, *_: (0, 0)),
        ),
    )(labels.reshape(-1), offset.reshape(1), diag_part.reshape(local_rows, 1), tiles)


def arrival_labels(
    row_map, col_map, child_size, groups, row_devs, col_devs, piece_rows, piece_cols,
    row_tiles, col_tiles, sentinel,
):
    children, side = row_map.shape[1], row_map.shape[2]
    span = children * side
    maps = jnp.concatenate(
        [row_map[0].reshape(-1), col_map[0].reshape(-1), child_size[0].reshape(-1)]
    )
    every = lax.all_gather(maps, "front")
    front_id = lax.axis_index("front")
    row_maps = every[:, :span].reshape(groups, children, side)[:, front_id]
    col_maps = every[:, span : 2 * span].reshape(groups, children, side)[:, front_id]
    sizes = every[:, 2 * span :].reshape(groups, children)[:, front_id]
    child_rows = (
        jnp.arange(row_devs, dtype=jnp.int32)[:, None] * piece_rows
        + jnp.arange(piece_rows, dtype=jnp.int32)[None, :]
    )
    child_cols = (
        jnp.arange(col_devs, dtype=jnp.int32)[:, None] * piece_cols
        + jnp.arange(piece_cols, dtype=jnp.int32)[None, :]
    )
    parent_rows = row_maps[:, child_rows]
    parent_cols = col_maps[:, child_cols]
    hit_rows = (child_rows[None] < sizes[:, None, None]) & (
        parent_rows // row_tiles == lax.axis_index("row")
    )
    hit_cols = (child_cols[None] < sizes[:, None, None]) & (
        parent_cols // col_tiles == lax.axis_index("column")
    )
    hit = hit_cols[:, :, None, None, :] & hit_rows[:, None, :, :, None]
    spot = (parent_rows % row_tiles)[:, None, :, :, None] * col_tiles + (
        parent_cols % col_tiles
    )[:, :, None, None, :]
    sources = groups * col_devs * row_devs
    hit = hit.reshape(sources, piece_rows * piece_cols).astype(jnp.int32)
    spot = jnp.broadcast_to(
        spot, (groups, col_devs, row_devs, piece_rows, piece_cols)
    ).reshape(sources, piece_rows * piece_cols)
    rank = jnp.cumsum(hit, axis=1) - hit
    slots = []
    for slot in range(ROWMOST):
        chosen = (hit == 1) & (rank == slot)
        slots.append(
            jnp.where(
                jnp.any(chosen, axis=1), jnp.sum(jnp.where(chosen, spot, 0), axis=1), sentinel
            )
        )
    return jnp.stack(slots, axis=1)


def body(cbs, row_map, col_map, child_size, front_diag, panel_order, pivot_inverse):
    groups = lax.axis_size("front")
    row_devs = lax.axis_size("row")
    col_devs = lax.axis_size("column")
    row_id = lax.axis_index("row")
    col_id = lax.axis_index("column")
    children = cbs.shape[1]
    piece_rows = cbs.shape[2] // TILE
    piece_cols = cbs.shape[3] // TILE
    local_rows = ORDER // row_devs
    local_cols = ORDER // col_devs
    row_tiles = local_rows // TILE
    col_tiles = local_cols // TILE
    sentinel = row_tiles * col_tiles
    tile_stack = (
        cbs[0].reshape(children, piece_rows, TILE, piece_cols, TILE).transpose(0, 1, 3, 2, 4)
    )
    tile_stack = tile_stack.reshape(-1, TILE, TILE)
    child_rows = row_id * piece_rows + jnp.arange(piece_rows, dtype=jnp.int32)
    child_cols = col_id * piece_cols + jnp.arange(piece_cols, dtype=jnp.int32)
    parent_rows = lax.dynamic_slice_in_dim(row_map[0], row_id * piece_rows, piece_rows, 1)
    parent_cols = lax.dynamic_slice_in_dim(col_map[0], col_id * piece_cols, piece_cols, 1)
    live_rows = child_rows[None, :] < child_size[0][:, None]
    live_cols = child_cols[None, :] < child_size[0][:, None]
    owner_rows = parent_rows // row_tiles
    owner_cols = parent_cols // col_tiles
    target_spot = (
        (parent_rows - owner_rows * row_tiles)[:, :, None] * col_tiles
        + (parent_cols - owner_cols * col_tiles)[:, None, :]
    ).reshape(-1)
    usable = (live_rows[:, :, None] & live_cols[:, None, :]).reshape(-1)
    inner_dest = (owner_cols[:, None, :] * row_devs + owner_rows[:, :, None]).reshape(-1)
    all_devices = groups * row_devs * col_devs
    front_ids = jnp.arange(children, dtype=jnp.int32)[:, None]
    whole_dest = (front_ids * (row_devs * col_devs) + inner_dest.reshape(children, -1)).reshape(-1)
    whole_target = jnp.where(usable, whole_dest, all_devices)
    payload, labels = pack_tiles(
        tile_stack, whole_target, target_spot, all_devices, ROWMOST, sentinel
    )
    arrived = lax.all_to_all(
        payload, ("front", "column", "row"), split_axis=0, concat_axis=0, tiled=True
    )
    arrived_labels = arrival_labels(
        row_map, col_map, child_size, groups, row_devs, col_devs, piece_rows, piece_cols,
        row_tiles, col_tiles, sentinel,
    )
    row_glob = row_id * local_rows + jnp.arange(local_rows, dtype=jnp.int32)
    col_glob = col_id * local_cols + jnp.arange(local_cols, dtype=jnp.int32)
    diag_part = lax.dynamic_slice_in_dim(front_diag[0], row_id * local_rows, local_rows)
    diag_offset = (row_id * local_rows - col_id * local_cols).astype(jnp.int32)
    matrix = scatter_tiles(arrived, arrived_labels, diag_part, diag_offset, local_rows, local_cols)
    order_row = panel_order[0]
    inverses = pivot_inverse[0]
    panel_rows = local_rows // PANEL
    panel_cols = local_cols // PANEL
    row_block = row_glob // PANEL
    col_block = col_glob // PANEL

    def strip_bounds(step_index):
        pivot_block = order_row[step_index]
        return (
            pivot_block // panel_cols,
            pivot_block // panel_rows,
            pivot_block % panel_cols * PANEL,
            pivot_block % panel_rows * PANEL,
        )

    def actives(step_index):
        chosen = order_row[: step_index + 1]
        active_rows = jnp.all(row_block[:, None] != chosen[None, :], axis=1)
        active_cols = jnp.all(col_block[:, None] != chosen[None, :], axis=1)
        return (active_rows, active_cols)

    def current_strips(matrix, step_index):
        col_owner, row_owner, col_offset, row_offset = strip_bounds(step_index)
        return (
            lax.dynamic_slice_in_dim(matrix, col_offset, PANEL, 1),
            lax.dynamic_slice_in_dim(matrix, row_offset, PANEL, 0),
        )

    def share_strips(col_strip, row_strip, step_index):
        col_owner, row_owner, col_offset, row_offset = strip_bounds(step_index)
        owner_left = jnp.dot(
            col_strip, inverses[step_index], precision=HIGHEST, preferred_element_type=jnp.float32
        )
        left_strip = exchange_broadcast(owner_left, "column", col_owner)
        top_strip = lax.psum(row_strip, "row")
        return (left_strip, top_strip)

    def owned_rows(row_strip, step_index):
        col_owner, row_owner, col_offset, row_offset = strip_bounds(step_index)
        return jnp.where(row_id == row_owner, row_strip, jnp.zeros_like(row_strip))

    first_col, first_row = current_strips(matrix, 0)
    left_strip, top_strip = share_strips(first_col, owned_rows(first_row, 0), 0)
    for step_index in range(PANELS):
        if step_index + 1 < PANELS:
            active_rows, active_cols = actives(step_index)
            next_col, next_row = current_strips(matrix, step_index + 1)
            col_owner, row_owner, col_offset, row_offset = strip_bounds(step_index + 1)
            top_part = lax.dynamic_slice_in_dim(top_strip, col_offset, PANEL, 1)
            left_part = lax.dynamic_slice_in_dim(left_strip, row_offset, PANEL, 0)
            next_row = jnp.where(
                active_cols[None, :],
                next_row
                - jnp.dot(
                    left_part, top_strip, precision=HIGHEST, preferred_element_type=jnp.float32
                ),
                next_row,
            )
            next_row = owned_rows(next_row, step_index + 1)
            next_row, next_col = lax.optimization_barrier((next_row, next_col))
            next_col = jnp.where(
                active_rows[:, None],
                next_col
                - jnp.dot(
                    left_strip, top_part, precision=HIGHEST, preferred_element_type=jnp.float32
                ),
                next_col,
            )
            left_next, top_next = share_strips(next_col, next_row, step_index + 1)
        eliminate_matrix = matrix
        eliminate_active_rows, eliminate_active_cols = actives(step_index)
        product = jnp.dot(
            left_strip, top_strip, precision=HIGHEST, preferred_element_type=jnp.float32
        )
        eliminate_matrix = jnp.where(
            eliminate_active_rows[:, None] & eliminate_active_cols[None, :],
            eliminate_matrix - product,
            eliminate_matrix,
        )
        eliminate_col_owner, eliminate_row_owner, eliminate_col_offset, eliminate_row_offset = (
            strip_bounds(step_index)
        )
        present = lax.dynamic_slice_in_dim(eliminate_matrix, eliminate_col_offset, PANEL, 1)
        fresh_col = jnp.where(
            (col_id == eliminate_col_owner) & eliminate_active_rows[:, None], left_strip, present
        )
        matrix = lax.dynamic_update_slice_in_dim(
            eliminate_matrix, fresh_col, eliminate_col_offset, 1
        )
        if step_index + 1 < PANELS:
            left_strip, top_strip = (left_next, top_next)
    return matrix[None]


def solution(mesh):
    placed = (
        P("front", None, "row", "column"),
        P("front", None, None),
        P("front", None, None),
        P("front", None),
        P("front", None),
        P("front", None),
        P("front", None, None, None),
    )
    return jax.shard_map(
        body, mesh=mesh, in_specs=placed, out_specs=P("front", "row", "column"), check_vma=False
    )
```

```python
import jax
import jax.numpy as jnp
from jax import lax
from jax.sharding import PartitionSpec as P
from jax.experimental import pallas as pl
from jax.experimental.pallas import tpu as pltpu

ORDER = 6144
TILE = 128
PANEL = 256
PANELS = 4
ROWMOST = 2


HIGHEST = lax.Precision.HIGHEST


def broadcast(block, axis, source):
    block = jnp.where(lax.axis_index(axis) == source, block, jnp.zeros_like(block))
    return lax.psum(block, axis)


def exchange_broadcast(block, axis, source):
    size = lax.axis_size(axis)
    if size & (size - 1):
        return broadcast(block, axis, source)
    index = lax.axis_index(axis)
    distance = 1
    while distance < size:
        partner = [(i, i ^ distance) for i in range(size)]
        received = lax.ppermute(block, axis, partner)
        take = (source // distance) % 2 != (index // distance) % 2
        block = jnp.where(take, received, block)
        distance *= 2
    return block


def pack_kernel(sources_ref, blocks_ref, out_ref):
    tile_side = out_ref.shape[-1]
    piece_rows = blocks_ref.shape[2] // tile_side
    piece_cols = blocks_ref.shape[3] // tile_side
    per_child = piece_rows * piece_cols

    def place(slot, carry):
        source = sources_ref[slot]

        @pl.when(source >= 0)
        def _():
            child = source // per_child
            row_start = pl.multiple_of((source // piece_cols) % piece_rows * tile_side, tile_side)
            col_start = pl.multiple_of(source % piece_cols * tile_side, tile_side)
            out_ref[slot] = blocks_ref[
                0, child, pl.ds(row_start, tile_side), pl.ds(col_start, tile_side)
            ]

        @pl.when(source < 0)
        def _():
            out_ref[slot] = jnp.zeros((tile_side, tile_side), out_ref.dtype)

        return carry

    lax.fori_loop(0, out_ref.shape[0], place, 0)


def pack_tiles(blocks, target_dev, dest_count, capacity):
    dest_iota = jnp.arange(dest_count, dtype=jnp.int32)
    matches = (target_dev[:, None] == dest_iota[None, :]).astype(jnp.int32)
    earlier = jnp.cumsum(matches, axis=0) - matches
    position = jnp.sum(earlier * matches, axis=1)
    usable = target_dev < dest_count
    slot_index = jnp.where(usable, target_dev * capacity + position, dest_count * capacity)
    tile_ids = jnp.arange(target_dev.shape[0], dtype=jnp.int32)
    sources = (
        jnp.full((dest_count * capacity,), -1, jnp.int32).at[slot_index].set(tile_ids, mode="drop")
    )
    slots = dest_count * capacity
    payload = pl.pallas_call(
        pack_kernel,
        out_shape=jax.ShapeDtypeStruct((slots, TILE, TILE), blocks.dtype),
        grid_spec=pltpu.PrefetchScalarGridSpec(
            num_scalar_prefetch=1,
            grid=(1,),
            in_specs=[pl.BlockSpec(blocks.shape, lambda i, *_: (0, 0, 0, 0))],
            out_specs=pl.BlockSpec((slots, TILE, TILE), lambda i, *_: (0, 0, 0)),
        ),
    )(sources, blocks)
    return payload.reshape((dest_count, capacity, TILE, TILE))


def assemble_kernel(spots_ref, offset_ref, diag_ref, payload_ref, out_ref):
    rows_total, cols_total = out_ref.shape
    tile_side = payload_ref.shape[-1]
    row_tiles = rows_total // tile_side
    col_tiles = cols_total // tile_side
    offset = offset_ref[0]
    for band in range(row_tiles):
        band_rows = pl.ds(band * tile_side, tile_side)
        row_iota = lax.broadcasted_iota(jnp.int32, (tile_side, cols_total), 0) + band * tile_side
        col_iota = lax.broadcasted_iota(jnp.int32, (tile_side, cols_total), 1)
        out_ref[band_rows, :] = jnp.where(
            row_iota + offset == col_iota, diag_ref[band_rows, :], 0.0
        )

    def add_tile(slot, carry):
        spot = spots_ref[slot]
        tile_row = spot // col_tiles
        tile_col = spot % col_tiles

        @pl.when(tile_row < row_tiles)
        def _():
            row_start = pl.multiple_of(tile_row * tile_side, tile_side)
            col_start = pl.multiple_of(tile_col * tile_side, tile_side)
            window = (pl.ds(row_start, tile_side), pl.ds(col_start, tile_side))
            out_ref[window] = out_ref[window] + payload_ref[slot]

        return carry

    lax.fori_loop(0, payload_ref.shape[0], add_tile, 0)


def scatter_tiles(payload, labels, diag_part, offset, local_rows, local_cols):
    tile_side = payload.shape[-1]
    tiles = payload.reshape(-1, tile_side, tile_side)
    slots = tiles.shape[0]
    return pl.pallas_call(
        assemble_kernel,
        out_shape=jax.ShapeDtypeStruct((local_rows, local_cols), jnp.float32),
        grid_spec=pltpu.PrefetchScalarGridSpec(
            num_scalar_prefetch=2,
            grid=(1,),
            in_specs=[
                pl.BlockSpec((local_rows, 1), lambda i, *_: (0, 0)),
                pl.BlockSpec((slots, tile_side, tile_side), lambda i, *_: (0, 0, 0)),
            ],
            out_specs=pl.BlockSpec((local_rows, local_cols), lambda i, *_: (0, 0)),
        ),
    )(labels.reshape(-1), offset.reshape(1), diag_part.reshape(local_rows, 1), tiles)


def arrival_labels(
    row_map, col_map, child_size, groups, row_devs, col_devs, piece_rows, piece_cols,
    row_tiles, col_tiles, sentinel,
):
    children, side = row_map.shape[1], row_map.shape[2]
    span = children * side
    maps = jnp.concatenate(
        [row_map[0].reshape(-1), col_map[0].reshape(-1), child_size[0].reshape(-1)]
    )
    every = lax.all_gather(maps, "front")
    front_id = lax.axis_index("front")
    row_maps = every[:, :span].reshape(groups, children, side)[:, front_id]
    col_maps = every[:, span : 2 * span].reshape(groups, children, side)[:, front_id]
    sizes = every[:, 2 * span :].reshape(groups, children)[:, front_id]
    child_rows = (
        jnp.arange(row_devs, dtype=jnp.int32)[:, None] * piece_rows
        + jnp.arange(piece_rows, dtype=jnp.int32)[None, :]
    )
    child_cols = (
        jnp.arange(col_devs, dtype=jnp.int32)[:, None] * piece_cols
        + jnp.arange(piece_cols, dtype=jnp.int32)[None, :]
    )
    parent_rows = row_maps[:, child_rows]
    parent_cols = col_maps[:, child_cols]
    hit_rows = (child_rows[None] < sizes[:, None, None]) & (
        parent_rows // row_tiles == lax.axis_index("row")
    )
    hit_cols = (child_cols[None] < sizes[:, None, None]) & (
        parent_cols // col_tiles == lax.axis_index("column")
    )
    hit = hit_cols[:, :, None, None, :] & hit_rows[:, None, :, :, None]
    spot = (parent_rows % row_tiles)[:, None, :, :, None] * col_tiles + (
        parent_cols % col_tiles
    )[:, :, None, None, :]
    sources = groups * col_devs * row_devs
    hit = hit.reshape(sources, piece_rows * piece_cols).astype(jnp.int32)
    spot = jnp.broadcast_to(
        spot, (groups, col_devs, row_devs, piece_rows, piece_cols)
    ).reshape(sources, piece_rows * piece_cols)
    rank = jnp.cumsum(hit, axis=1) - hit
    slots = []
    for slot in range(ROWMOST):
        chosen = (hit == 1) & (rank == slot)
        slots.append(
            jnp.where(
                jnp.any(chosen, axis=1), jnp.sum(jnp.where(chosen, spot, 0), axis=1), sentinel
            )
        )
    return jnp.stack(slots, axis=1)


def body(cbs, row_map, col_map, child_size, front_diag, panel_order, pivot_inverse):
    groups = lax.axis_size("front")
    row_devs = lax.axis_size("row")
    col_devs = lax.axis_size("column")
    row_id = lax.axis_index("row")
    col_id = lax.axis_index("column")
    children = cbs.shape[1]
    piece_rows = cbs.shape[2] // TILE
    piece_cols = cbs.shape[3] // TILE
    local_rows = ORDER // row_devs
    local_cols = ORDER // col_devs
    row_tiles = local_rows // TILE
    col_tiles = local_cols // TILE
    sentinel = row_tiles * col_tiles
    child_rows = row_id * piece_rows + jnp.arange(piece_rows, dtype=jnp.int32)
    child_cols = col_id * piece_cols + jnp.arange(piece_cols, dtype=jnp.int32)
    parent_rows = lax.dynamic_slice_in_dim(row_map[0], row_id * piece_rows, piece_rows, 1)
    parent_cols = lax.dynamic_slice_in_dim(col_map[0], col_id * piece_cols, piece_cols, 1)
    live_rows = child_rows[None, :] < child_size[0][:, None]
    live_cols = child_cols[None, :] < child_size[0][:, None]
    owner_rows = parent_rows // row_tiles
    owner_cols = parent_cols // col_tiles
    target_spot = (
        (parent_rows - owner_rows * row_tiles)[:, :, None] * col_tiles
        + (parent_cols - owner_cols * col_tiles)[:, None, :]
    ).reshape(-1)
    usable = (live_rows[:, :, None] & live_cols[:, None, :]).reshape(-1)
    inner_dest = (owner_cols[:, None, :] * row_devs + owner_rows[:, :, None]).reshape(-1)
    all_devices = groups * row_devs * col_devs
    front_ids = jnp.arange(children, dtype=jnp.int32)[:, None]
    whole_dest = (front_ids * (row_devs * col_devs) + inner_dest.reshape(children, -1)).reshape(-1)
    whole_target = jnp.where(usable, whole_dest, all_devices)
    payload = pack_tiles(cbs, whole_target, all_devices, ROWMOST)
    arrived = lax.all_to_all(
        payload, ("front", "column", "row"), split_axis=0, concat_axis=0, tiled=True
    )
    arrived_labels = arrival_labels(
        row_map, col_map, child_size, groups, row_devs, col_devs, piece_rows, piece_cols,
        row_tiles, col_tiles, sentinel,
    )
    row_glob = row_id * local_rows + jnp.arange(local_rows, dtype=jnp.int32)
    col_glob = col_id * local_cols + jnp.arange(local_cols, dtype=jnp.int32)
    diag_part = lax.dynamic_slice_in_dim(front_diag[0], row_id * local_rows, local_rows)
    diag_offset = (row_id * local_rows - col_id * local_cols).astype(jnp.int32)
    matrix = scatter_tiles(arrived, arrived_labels, diag_part, diag_offset, local_rows, local_cols)
    order_row = panel_order[0]
    inverses = pivot_inverse[0]
    panel_rows = local_rows // PANEL
    panel_cols = local_cols // PANEL
    row_block = row_glob // PANEL
    col_block = col_glob // PANEL

    def strip_bounds(step_index):
        pivot_block = order_row[step_index]
        return (
            pivot_block // panel_cols,
            pivot_block // panel_rows,
            pivot_block % panel_cols * PANEL,
            pivot_block % panel_rows * PANEL,
        )

    def actives(step_index):
        chosen = order_row[: step_index + 1]
        active_rows = jnp.all(row_block[:, None] != chosen[None, :], axis=1)
        active_cols = jnp.all(col_block[:, None] != chosen[None, :], axis=1)
        return (active_rows, active_cols)

    def current_strips(matrix, step_index):
        col_owner, row_owner, col_offset, row_offset = strip_bounds(step_index)
        return (
            lax.dynamic_slice_in_dim(matrix, col_offset, PANEL, 1),
            lax.dynamic_slice_in_dim(matrix, row_offset, PANEL, 0),
        )

    def share_strips(col_strip, row_strip, step_index):
        col_owner, row_owner, col_offset, row_offset = strip_bounds(step_index)
        owner_left = jnp.dot(
            col_strip, inverses[step_index], precision=HIGHEST, preferred_element_type=jnp.float32
        )
        left_strip = exchange_broadcast(owner_left, "column", col_owner)
        top_strip = lax.psum(row_strip, "row")
        return (left_strip, top_strip)

    def owned_rows(row_strip, step_index):
        col_owner, row_owner, col_offset, row_offset = strip_bounds(step_index)
        return jnp.where(row_id == row_owner, row_strip, jnp.zeros_like(row_strip))

    first_col, first_row = current_strips(matrix, 0)
    left_strip, top_strip = share_strips(first_col, owned_rows(first_row, 0), 0)
    for step_index in range(PANELS):
        if step_index + 1 < PANELS:
            active_rows, active_cols = actives(step_index)
            next_col, next_row = current_strips(matrix, step_index + 1)
            col_owner, row_owner, col_offset, row_offset = strip_bounds(step_index + 1)
            top_part = lax.dynamic_slice_in_dim(top_strip, col_offset, PANEL, 1)
            left_part = lax.dynamic_slice_in_dim(left_strip, row_offset, PANEL, 0)
            next_row = jnp.where(
                active_cols[None, :],
                next_row
                - jnp.dot(
                    left_part, top_strip, precision=HIGHEST, preferred_element_type=jnp.float32
                ),
                next_row,
            )
            next_row = owned_rows(next_row, step_index + 1)
            next_row, next_col = lax.optimization_barrier((next_row, next_col))
            next_col = jnp.where(
                active_rows[:, None],
                next_col
                - jnp.dot(
                    left_strip, top_part, precision=HIGHEST, preferred_element_type=jnp.float32
                ),
                next_col,
            )
            left_next, top_next = share_strips(next_col, next_row, step_index + 1)
        eliminate_matrix = matrix
        eliminate_active_rows, eliminate_active_cols = actives(step_index)
        product = jnp.dot(
            left_strip, top_strip, precision=HIGHEST, preferred_element_type=jnp.float32
        )
        eliminate_matrix = jnp.where(
            eliminate_active_rows[:, None] & eliminate_active_cols[None, :],
            eliminate_matrix - product,
            eliminate_matrix,
        )
        eliminate_col_owner, eliminate_row_owner, eliminate_col_offset, eliminate_row_offset = (
            strip_bounds(step_index)
        )
        present = lax.dynamic_slice_in_dim(eliminate_matrix, eliminate_col_offset, PANEL, 1)
        fresh_col = jnp.where(
            (col_id == eliminate_col_owner) & eliminate_active_rows[:, None], left_strip, present
        )
        matrix = lax.dynamic_update_slice_in_dim(
            eliminate_matrix, fresh_col, eliminate_col_offset, 1
        )
        if step_index + 1 < PANELS:
            left_strip, top_strip = (left_next, top_next)
    return matrix[None]


def solution(mesh):
    placed = (
        P("front", None, "row", "column"),
        P("front", None, None),
        P("front", None, None),
        P("front", None),
        P("front", None),
        P("front", None),
        P("front", None, None, None),
    )
    return jax.shard_map(
        body, mesh=mesh, in_specs=placed, out_specs=P("front", "row", "column"), check_vma=False
    )
```

```python
import jax
import jax.numpy as jnp
from jax import lax
from jax.sharding import PartitionSpec as P
from jax.experimental import pallas as pl
from jax.experimental.pallas import tpu as pltpu

ORDER = 6144
TILE = 128
PANEL = 256
PANELS = 4
ROWMOST = 2


HIGHEST = lax.Precision.HIGHEST


def broadcast(block, axis, source):
    block = jnp.where(lax.axis_index(axis) == source, block, jnp.zeros_like(block))
    return lax.psum(block, axis)


def exchange_broadcast(block, axis, source):
    size = lax.axis_size(axis)
    if size & (size - 1):
        return broadcast(block, axis, source)
    index = lax.axis_index(axis)
    distance = 1
    while distance < size:
        partner = [(i, i ^ distance) for i in range(size)]
        received = lax.ppermute(block, axis, partner)
        take = (source // distance) % 2 != (index // distance) % 2
        block = jnp.where(take, received, block)
        distance *= 2
    return block


def pack_kernel(sources_ref, blocks_ref, out_ref):
    tile_side = out_ref.shape[-1]
    piece_rows = blocks_ref.shape[2] // tile_side
    piece_cols = blocks_ref.shape[3] // tile_side
    per_child = piece_rows * piece_cols

    def place(slot, carry):
        source = sources_ref[slot]

        @pl.when(source >= 0)
        def _():
            child = source // per_child
            row_start = pl.multiple_of((source // piece_cols) % piece_rows * tile_side, tile_side)
            col_start = pl.multiple_of(source % piece_cols * tile_side, tile_side)
            out_ref[slot] = blocks_ref[
                0, child, pl.ds(row_start, tile_side), pl.ds(col_start, tile_side)
            ]

        @pl.when(source < 0)
        def _():
            out_ref[slot] = jnp.zeros((tile_side, tile_side), out_ref.dtype)

        return carry

    lax.fori_loop(0, out_ref.shape[0], place, 0)


def pack_tiles(blocks, target_dev, dest_count, capacity):
    dest_iota = jnp.arange(dest_count, dtype=jnp.int32)
    matches = (target_dev[:, None] == dest_iota[None, :]).astype(jnp.int32)
    earlier = jnp.cumsum(matches, axis=0) - matches
    position = jnp.sum(earlier * matches, axis=1)
    usable = target_dev < dest_count
    slot_index = jnp.where(usable, target_dev * capacity + position, dest_count * capacity)
    tile_ids = jnp.arange(target_dev.shape[0], dtype=jnp.int32)
    sources = (
        jnp.full((dest_count * capacity,), -1, jnp.int32).at[slot_index].set(tile_ids, mode="drop")
    )
    slots = dest_count * capacity
    payload = pl.pallas_call(
        pack_kernel,
        out_shape=jax.ShapeDtypeStruct((slots, TILE, TILE), blocks.dtype),
        grid_spec=pltpu.PrefetchScalarGridSpec(
            num_scalar_prefetch=1,
            grid=(1,),
            in_specs=[pl.BlockSpec(blocks.shape, lambda i, *_: (0, 0, 0, 0))],
            out_specs=pl.BlockSpec((slots, TILE, TILE), lambda i, *_: (0, 0, 0)),
        ),
    )(sources, blocks)
    return payload.reshape((dest_count, capacity, TILE, TILE))


def assemble_kernel(spots_ref, offset_ref, diag_ref, payload_ref, out_ref):
    band_rows, cols_total = out_ref.shape
    tile_side = payload_ref.shape[-1]
    col_tiles = cols_total // tile_side
    band = pl.program_id(0)
    row_iota = lax.broadcasted_iota(jnp.int32, (band_rows, cols_total), 0) + band * band_rows
    col_iota = lax.broadcasted_iota(jnp.int32, (band_rows, cols_total), 1)
    out_ref[...] = jnp.where(row_iota + offset_ref[0] == col_iota, diag_ref[...], 0.0)

    def add_tile(slot, carry):
        spot = spots_ref[slot]

        @pl.when(spot // col_tiles == band)
        def _():
            col_start = pl.multiple_of(spot % col_tiles * tile_side, tile_side)
            window = (slice(None), pl.ds(col_start, tile_side))
            out_ref[window] = out_ref[window] + payload_ref[slot]

        return carry

    lax.fori_loop(0, payload_ref.shape[0], add_tile, 0)


def scatter_tiles(payload, labels, diag_part, offset, local_rows, local_cols):
    tile_side = payload.shape[-1]
    tiles = payload.reshape(-1, tile_side, tile_side)
    slots = tiles.shape[0]
    return pl.pallas_call(
        assemble_kernel,
        out_shape=jax.ShapeDtypeStruct((local_rows, local_cols), jnp.float32),
        grid_spec=pltpu.PrefetchScalarGridSpec(
            num_scalar_prefetch=2,
            grid=(local_rows // tile_side,),
            in_specs=[
                pl.BlockSpec((tile_side, 1), lambda i, *_: (i, 0)),
                pl.BlockSpec((slots, tile_side, tile_side), lambda i, *_: (0, 0, 0)),
            ],
            out_specs=pl.BlockSpec((tile_side, local_cols), lambda i, *_: (i, 0)),
        ),
    )(labels.reshape(-1), offset.reshape(1), diag_part.reshape(local_rows, 1), tiles)


def arrival_labels(
    row_map, col_map, child_size, groups, row_devs, col_devs, piece_rows, piece_cols,
    row_tiles, col_tiles, sentinel,
):
    children, side = row_map.shape[1], row_map.shape[2]
    span = children * side
    maps = jnp.concatenate(
        [row_map[0].reshape(-1), col_map[0].reshape(-1), child_size[0].reshape(-1)]
    )
    every = lax.all_gather(maps, "front")
    front_id = lax.axis_index("front")
    row_maps = every[:, :span].reshape(groups, children, side)[:, front_id]
    col_maps = every[:, span : 2 * span].reshape(groups, children, side)[:, front_id]
    sizes = every[:, 2 * span :].reshape(groups, children)[:, front_id]
    child_rows = (
        jnp.arange(row_devs, dtype=jnp.int32)[:, None] * piece_rows
        + jnp.arange(piece_rows, dtype=jnp.int32)[None, :]
    )
    child_cols = (
        jnp.arange(col_devs, dtype=jnp.int32)[:, None] * piece_cols
        + jnp.arange(piece_cols, dtype=jnp.int32)[None, :]
    )
    parent_rows = row_maps[:, child_rows]
    parent_cols = col_maps[:, child_cols]
    hit_rows = (child_rows[None] < sizes[:, None, None]) & (
        parent_rows // row_tiles == lax.axis_index("row")
    )
    hit_cols = (child_cols[None] < sizes[:, None, None]) & (
        parent_cols // col_tiles == lax.axis_index("column")
    )
    hit = hit_cols[:, :, None, None, :] & hit_rows[:, None, :, :, None]
    spot = (parent_rows % row_tiles)[:, None, :, :, None] * col_tiles + (
        parent_cols % col_tiles
    )[:, :, None, None, :]
    sources = groups * col_devs * row_devs
    hit = hit.reshape(sources, piece_rows * piece_cols).astype(jnp.int32)
    spot = jnp.broadcast_to(
        spot, (groups, col_devs, row_devs, piece_rows, piece_cols)
    ).reshape(sources, piece_rows * piece_cols)
    rank = jnp.cumsum(hit, axis=1) - hit
    slots = []
    for slot in range(ROWMOST):
        chosen = (hit == 1) & (rank == slot)
        slots.append(
            jnp.where(
                jnp.any(chosen, axis=1), jnp.sum(jnp.where(chosen, spot, 0), axis=1), sentinel
            )
        )
    return jnp.stack(slots, axis=1)


def body(cbs, row_map, col_map, child_size, front_diag, panel_order, pivot_inverse):
    groups = lax.axis_size("front")
    row_devs = lax.axis_size("row")
    col_devs = lax.axis_size("column")
    row_id = lax.axis_index("row")
    col_id = lax.axis_index("column")
    children = cbs.shape[1]
    piece_rows = cbs.shape[2] // TILE
    piece_cols = cbs.shape[3] // TILE
    local_rows = ORDER // row_devs
    local_cols = ORDER // col_devs
    row_tiles = local_rows // TILE
    col_tiles = local_cols // TILE
    sentinel = row_tiles * col_tiles
    child_rows = row_id * piece_rows + jnp.arange(piece_rows, dtype=jnp.int32)
    child_cols = col_id * piece_cols + jnp.arange(piece_cols, dtype=jnp.int32)
    parent_rows = lax.dynamic_slice_in_dim(row_map[0], row_id * piece_rows, piece_rows, 1)
    parent_cols = lax.dynamic_slice_in_dim(col_map[0], col_id * piece_cols, piece_cols, 1)
    live_rows = child_rows[None, :] < child_size[0][:, None]
    live_cols = child_cols[None, :] < child_size[0][:, None]
    owner_rows = parent_rows // row_tiles
    owner_cols = parent_cols // col_tiles
    target_spot = (
        (parent_rows - owner_rows * row_tiles)[:, :, None] * col_tiles
        + (parent_cols - owner_cols * col_tiles)[:, None, :]
    ).reshape(-1)
    usable = (live_rows[:, :, None] & live_cols[:, None, :]).reshape(-1)
    inner_dest = (owner_cols[:, None, :] * row_devs + owner_rows[:, :, None]).reshape(-1)
    all_devices = groups * row_devs * col_devs
    front_ids = jnp.arange(children, dtype=jnp.int32)[:, None]
    whole_dest = (front_ids * (row_devs * col_devs) + inner_dest.reshape(children, -1)).reshape(-1)
    whole_target = jnp.where(usable, whole_dest, all_devices)
    payload = pack_tiles(cbs, whole_target, all_devices, ROWMOST)
    arrived = lax.all_to_all(
        payload, ("front", "column", "row"), split_axis=0, concat_axis=0, tiled=True
    )
    arrived_labels = arrival_labels(
        row_map, col_map, child_size, groups, row_devs, col_devs, piece_rows, piece_cols,
        row_tiles, col_tiles, sentinel,
    )
    row_glob = row_id * local_rows + jnp.arange(local_rows, dtype=jnp.int32)
    col_glob = col_id * local_cols + jnp.arange(local_cols, dtype=jnp.int32)
    diag_part = lax.dynamic_slice_in_dim(front_diag[0], row_id * local_rows, local_rows)
    diag_offset = (row_id * local_rows - col_id * local_cols).astype(jnp.int32)
    matrix = scatter_tiles(arrived, arrived_labels, diag_part, diag_offset, local_rows, local_cols)
    order_row = panel_order[0]
    inverses = pivot_inverse[0]
    panel_rows = local_rows // PANEL
    panel_cols = local_cols // PANEL
    row_block = row_glob // PANEL
    col_block = col_glob // PANEL

    def strip_bounds(step_index):
        pivot_block = order_row[step_index]
        return (
            pivot_block // panel_cols,
            pivot_block // panel_rows,
            pivot_block % panel_cols * PANEL,
            pivot_block % panel_rows * PANEL,
        )

    def actives(step_index):
        chosen = order_row[: step_index + 1]
        active_rows = jnp.all(row_block[:, None] != chosen[None, :], axis=1)
        active_cols = jnp.all(col_block[:, None] != chosen[None, :], axis=1)
        return (active_rows, active_cols)

    def current_strips(matrix, step_index):
        col_owner, row_owner, col_offset, row_offset = strip_bounds(step_index)
        return (
            lax.dynamic_slice_in_dim(matrix, col_offset, PANEL, 1),
            lax.dynamic_slice_in_dim(matrix, row_offset, PANEL, 0),
        )

    def share_strips(col_strip, row_strip, step_index):
        col_owner, row_owner, col_offset, row_offset = strip_bounds(step_index)
        owner_left = jnp.dot(
            col_strip, inverses[step_index], precision=HIGHEST, preferred_element_type=jnp.float32
        )
        left_strip = exchange_broadcast(owner_left, "column", col_owner)
        top_strip = lax.psum(row_strip, "row")
        return (left_strip, top_strip)

    def owned_rows(row_strip, step_index):
        col_owner, row_owner, col_offset, row_offset = strip_bounds(step_index)
        return jnp.where(row_id == row_owner, row_strip, jnp.zeros_like(row_strip))

    first_col, first_row = current_strips(matrix, 0)
    first_row = owned_rows(first_row, 0)
    first_row, first_col = lax.optimization_barrier((first_row, first_col))
    left_strip, top_strip = share_strips(first_col, first_row, 0)
    for step_index in range(PANELS):
        if step_index + 1 < PANELS:
            active_rows, active_cols = actives(step_index)
            next_col, next_row = current_strips(matrix, step_index + 1)
            col_owner, row_owner, col_offset, row_offset = strip_bounds(step_index + 1)
            top_part = lax.dynamic_slice_in_dim(top_strip, col_offset, PANEL, 1)
            left_part = lax.dynamic_slice_in_dim(left_strip, row_offset, PANEL, 0)
            next_row = jnp.where(
                active_cols[None, :],
                next_row
                - jnp.dot(
                    left_part, top_strip, precision=HIGHEST, preferred_element_type=jnp.float32
                ),
                next_row,
            )
            next_row = owned_rows(next_row, step_index + 1)
            next_row, next_col = lax.optimization_barrier((next_row, next_col))
            next_col = jnp.where(
                active_rows[:, None],
                next_col
                - jnp.dot(
                    left_strip, top_part, precision=HIGHEST, preferred_element_type=jnp.float32
                ),
                next_col,
            )
            left_next, top_next = share_strips(next_col, next_row, step_index + 1)
        eliminate_matrix = matrix
        eliminate_active_rows, eliminate_active_cols = actives(step_index)
        product = jnp.dot(
            left_strip, top_strip, precision=HIGHEST, preferred_element_type=jnp.float32
        )
        eliminate_matrix = jnp.where(
            eliminate_active_rows[:, None] & eliminate_active_cols[None, :],
            eliminate_matrix - product,
            eliminate_matrix,
        )
        eliminate_col_owner, eliminate_row_owner, eliminate_col_offset, eliminate_row_offset = (
            strip_bounds(step_index)
        )
        present = lax.dynamic_slice_in_dim(eliminate_matrix, eliminate_col_offset, PANEL, 1)
        fresh_col = jnp.where(
            (col_id == eliminate_col_owner) & eliminate_active_rows[:, None], left_strip, present
        )
        matrix = lax.dynamic_update_slice_in_dim(
            eliminate_matrix, fresh_col, eliminate_col_offset, 1
        )
        if step_index + 1 < PANELS:
            left_strip, top_strip = (left_next, top_next)
    return matrix[None]


def solution(mesh):
    placed = (
        P("front", None, "row", "column"),
        P("front", None, None),
        P("front", None, None),
        P("front", None),
        P("front", None),
        P("front", None),
        P("front", None, None, None),
    )
    return jax.shard_map(
        body, mesh=mesh, in_specs=placed, out_specs=P("front", "row", "column"), check_vma=False
    )
```

```python
import jax
import jax.numpy as jnp
from jax import lax
from jax.sharding import PartitionSpec as P
from jax.experimental import pallas as pl
from jax.experimental.pallas import tpu as pltpu

ORDER = 6144
TILE = 128
PANEL = 256
PANELS = 4
ROWMOST = 2


HIGHEST = lax.Precision.HIGHEST


def broadcast(block, axis, source):
    block = jnp.where(lax.axis_index(axis) == source, block, jnp.zeros_like(block))
    return lax.psum(block, axis)


def exchange_broadcast(block, axis, source):
    size = lax.axis_size(axis)
    if size & (size - 1):
        return broadcast(block, axis, source)
    index = lax.axis_index(axis)
    distance = 1
    while distance < size:
        partner = [(i, i ^ distance) for i in range(size)]
        received = lax.ppermute(block, axis, partner)
        take = (source // distance) % 2 != (index // distance) % 2
        block = jnp.where(take, received, block)
        distance *= 2
    return block


def pack_kernel(sources_ref, blocks_ref, out_ref):
    tile_side = out_ref.shape[-1]
    piece_rows = blocks_ref.shape[2] // tile_side
    piece_cols = blocks_ref.shape[3] // tile_side
    per_child = piece_rows * piece_cols

    def place(slot, carry):
        source = sources_ref[slot]

        @pl.when(source >= 0)
        def _():
            child = source // per_child
            row_start = pl.multiple_of((source // piece_cols) % piece_rows * tile_side, tile_side)
            col_start = pl.multiple_of(source % piece_cols * tile_side, tile_side)
            out_ref[slot] = blocks_ref[
                0, child, pl.ds(row_start, tile_side), pl.ds(col_start, tile_side)
            ]

        @pl.when(source < 0)
        def _():
            out_ref[slot] = jnp.zeros((tile_side, tile_side), out_ref.dtype)

        return carry

    lax.fori_loop(0, out_ref.shape[0], place, 0)


def pack_tiles(blocks, target_dev, dest_count, capacity):
    dest_iota = jnp.arange(dest_count, dtype=jnp.int32)
    matches = (target_dev[:, None] == dest_iota[None, :]).astype(jnp.int32)
    earlier = jnp.cumsum(matches, axis=0) - matches
    position = jnp.sum(earlier * matches, axis=1)
    usable = target_dev < dest_count
    slot_index = jnp.where(usable, target_dev * capacity + position, dest_count * capacity)
    tile_ids = jnp.arange(target_dev.shape[0], dtype=jnp.int32)
    sources = (
        jnp.full((dest_count * capacity,), -1, jnp.int32).at[slot_index].set(tile_ids, mode="drop")
    )
    slots = dest_count * capacity
    payload = pl.pallas_call(
        pack_kernel,
        out_shape=jax.ShapeDtypeStruct((slots, TILE, TILE), blocks.dtype),
        grid_spec=pltpu.PrefetchScalarGridSpec(
            num_scalar_prefetch=1,
            grid=(1,),
            in_specs=[pl.BlockSpec(blocks.shape, lambda i, *_: (0, 0, 0, 0))],
            out_specs=pl.BlockSpec((slots, TILE, TILE), lambda i, *_: (0, 0, 0)),
        ),
    )(sources, blocks)
    return payload.reshape((dest_count, capacity, TILE, TILE))


def assemble_kernel(spots_ref, offset_ref, diag_ref, payload_ref, out_ref):
    rows_total, cols_total = out_ref.shape
    tile_side = payload_ref.shape[-1]
    row_tiles = rows_total // tile_side
    col_tiles = cols_total // tile_side
    offset = offset_ref[0]
    for band in range(row_tiles):
        band_rows = pl.ds(band * tile_side, tile_side)
        row_iota = lax.broadcasted_iota(jnp.int32, (tile_side, cols_total), 0) + band * tile_side
        col_iota = lax.broadcasted_iota(jnp.int32, (tile_side, cols_total), 1)
        out_ref[band_rows, :] = jnp.where(
            row_iota + offset == col_iota, diag_ref[band_rows, :], 0.0
        )

    def add_tile(slot, carry):
        spot = spots_ref[slot]
        tile_row = spot // col_tiles
        tile_col = spot % col_tiles

        @pl.when(tile_row < row_tiles)
        def _():
            row_start = pl.multiple_of(tile_row * tile_side, tile_side)
            col_start = pl.multiple_of(tile_col * tile_side, tile_side)
            window = (pl.ds(row_start, tile_side), pl.ds(col_start, tile_side))
            out_ref[window] = out_ref[window] + payload_ref[slot]

        return carry

    lax.fori_loop(0, payload_ref.shape[0], add_tile, 0)


def scatter_tiles(payload, labels, diag_part, offset, local_rows, local_cols):
    tile_side = payload.shape[-1]
    tiles = payload.reshape(-1, tile_side, tile_side)
    slots = tiles.shape[0]
    return pl.pallas_call(
        assemble_kernel,
        out_shape=jax.ShapeDtypeStruct((local_rows, local_cols), jnp.float32),
        grid_spec=pltpu.PrefetchScalarGridSpec(
            num_scalar_prefetch=2,
            grid=(1,),
            in_specs=[
                pl.BlockSpec((local_rows, 1), lambda i, *_: (0, 0)),
                pl.BlockSpec((slots, tile_side, tile_side), lambda i, *_: (0, 0, 0)),
            ],
            out_specs=pl.BlockSpec((local_rows, local_cols), lambda i, *_: (0, 0)),
        ),
    )(labels.reshape(-1), offset.reshape(1), diag_part.reshape(local_rows, 1), tiles)


def arrival_labels(
    row_map, col_map, child_size, groups, row_devs, col_devs, piece_rows, piece_cols,
    row_tiles, col_tiles, sentinel,
):
    children, side = row_map.shape[1], row_map.shape[2]
    span = children * side
    maps = jnp.concatenate(
        [row_map[0].reshape(-1), col_map[0].reshape(-1), child_size[0].reshape(-1)]
    )
    every = lax.all_gather(maps, "front")
    front_id = lax.axis_index("front")
    row_maps = every[:, :span].reshape(groups, children, side)[:, front_id]
    col_maps = every[:, span : 2 * span].reshape(groups, children, side)[:, front_id]
    sizes = every[:, 2 * span :].reshape(groups, children)[:, front_id]
    child_rows = (
        jnp.arange(row_devs, dtype=jnp.int32)[:, None] * piece_rows
        + jnp.arange(piece_rows, dtype=jnp.int32)[None, :]
    )
    child_cols = (
        jnp.arange(col_devs, dtype=jnp.int32)[:, None] * piece_cols
        + jnp.arange(piece_cols, dtype=jnp.int32)[None, :]
    )
    parent_rows = row_maps[:, child_rows]
    parent_cols = col_maps[:, child_cols]
    hit_rows = (child_rows[None] < sizes[:, None, None]) & (
        parent_rows // row_tiles == lax.axis_index("row")
    )
    hit_cols = (child_cols[None] < sizes[:, None, None]) & (
        parent_cols // col_tiles == lax.axis_index("column")
    )
    hit = hit_cols[:, :, None, None, :] & hit_rows[:, None, :, :, None]
    spot = (parent_rows % row_tiles)[:, None, :, :, None] * col_tiles + (
        parent_cols % col_tiles
    )[:, :, None, None, :]
    sources = groups * col_devs * row_devs
    hit = hit.reshape(sources, piece_rows * piece_cols).astype(jnp.int32)
    spot = jnp.broadcast_to(
        spot, (groups, col_devs, row_devs, piece_rows, piece_cols)
    ).reshape(sources, piece_rows * piece_cols)
    rank = jnp.cumsum(hit, axis=1) - hit
    slots = []
    for slot in range(ROWMOST):
        chosen = (hit == 1) & (rank == slot)
        slots.append(
            jnp.where(
                jnp.any(chosen, axis=1), jnp.sum(jnp.where(chosen, spot, 0), axis=1), sentinel
            )
        )
    return jnp.stack(slots, axis=1)


def body(cbs, row_map, col_map, child_size, front_diag, panel_order, pivot_inverse):
    groups = lax.axis_size("front")
    row_devs = lax.axis_size("row")
    col_devs = lax.axis_size("column")
    row_id = lax.axis_index("row")
    col_id = lax.axis_index("column")
    children = cbs.shape[1]
    piece_rows = cbs.shape[2] // TILE
    piece_cols = cbs.shape[3] // TILE
    local_rows = ORDER // row_devs
    local_cols = ORDER // col_devs
    row_tiles = local_rows // TILE
    col_tiles = local_cols // TILE
    sentinel = row_tiles * col_tiles
    child_rows = row_id * piece_rows + jnp.arange(piece_rows, dtype=jnp.int32)
    child_cols = col_id * piece_cols + jnp.arange(piece_cols, dtype=jnp.int32)
    parent_rows = lax.dynamic_slice_in_dim(row_map[0], row_id * piece_rows, piece_rows, 1)
    parent_cols = lax.dynamic_slice_in_dim(col_map[0], col_id * piece_cols, piece_cols, 1)
    live_rows = child_rows[None, :] < child_size[0][:, None]
    live_cols = child_cols[None, :] < child_size[0][:, None]
    owner_rows = parent_rows // row_tiles
    owner_cols = parent_cols // col_tiles
    target_spot = (
        (parent_rows - owner_rows * row_tiles)[:, :, None] * col_tiles
        + (parent_cols - owner_cols * col_tiles)[:, None, :]
    ).reshape(-1)
    usable = (live_rows[:, :, None] & live_cols[:, None, :]).reshape(-1)
    inner_dest = (owner_cols[:, None, :] * row_devs + owner_rows[:, :, None]).reshape(-1)
    all_devices = groups * row_devs * col_devs
    front_ids = jnp.arange(children, dtype=jnp.int32)[:, None]
    whole_dest = (front_ids * (row_devs * col_devs) + inner_dest.reshape(children, -1)).reshape(-1)
    whole_target = jnp.where(usable, whole_dest, all_devices)
    payload = pack_tiles(cbs, whole_target, all_devices, ROWMOST)
    arrived = lax.all_to_all(
        payload, ("front", "column", "row"), split_axis=0, concat_axis=0, tiled=True
    )
    arrived_labels = arrival_labels(
        row_map, col_map, child_size, groups, row_devs, col_devs, piece_rows, piece_cols,
        row_tiles, col_tiles, sentinel,
    )
    row_glob = row_id * local_rows + jnp.arange(local_rows, dtype=jnp.int32)
    col_glob = col_id * local_cols + jnp.arange(local_cols, dtype=jnp.int32)
    diag_part = lax.dynamic_slice_in_dim(front_diag[0], row_id * local_rows, local_rows)
    diag_offset = (row_id * local_rows - col_id * local_cols).astype(jnp.int32)
    matrix = scatter_tiles(arrived, arrived_labels, diag_part, diag_offset, local_rows, local_cols)
    order_row = panel_order[0]
    inverses = pivot_inverse[0]
    panel_rows = local_rows // PANEL
    panel_cols = local_cols // PANEL
    row_block = row_glob // PANEL
    col_block = col_glob // PANEL

    def strip_bounds(step_index):
        pivot_block = order_row[step_index]
        return (
            pivot_block // panel_cols,
            pivot_block // panel_rows,
            pivot_block % panel_cols * PANEL,
            pivot_block % panel_rows * PANEL,
        )

    def actives(step_index):
        chosen = order_row[: step_index + 1]
        active_rows = jnp.all(row_block[:, None] != chosen[None, :], axis=1)
        active_cols = jnp.all(col_block[:, None] != chosen[None, :], axis=1)
        return (active_rows, active_cols)

    def current_strips(matrix, step_index):
        col_owner, row_owner, col_offset, row_offset = strip_bounds(step_index)
        return (
            lax.dynamic_slice_in_dim(matrix, col_offset, PANEL, 1),
            lax.dynamic_slice_in_dim(matrix, row_offset, PANEL, 0),
        )

    def share_strips(col_strip, row_strip, step_index):
        col_owner, row_owner, col_offset, row_offset = strip_bounds(step_index)
        owner_left = jnp.dot(
            col_strip, inverses[step_index], precision=HIGHEST, preferred_element_type=jnp.float32
        )
        left_strip = exchange_broadcast(owner_left, "column", col_owner)
        top_strip = lax.psum(row_strip, "row")
        return (left_strip, top_strip)

    def owned_rows(row_strip, step_index):
        col_owner, row_owner, col_offset, row_offset = strip_bounds(step_index)
        return jnp.where(row_id == row_owner, row_strip, jnp.zeros_like(row_strip))

    first_col, first_row = current_strips(matrix, 0)
    left_strip, top_strip = share_strips(first_col, owned_rows(first_row, 0), 0)
    for step_index in range(PANELS):
        if step_index + 1 < PANELS:
            active_rows, active_cols = actives(step_index)
            next_col, next_row = current_strips(matrix, step_index + 1)
            col_owner, row_owner, col_offset, row_offset = strip_bounds(step_index + 1)
            top_part = lax.dynamic_slice_in_dim(top_strip, col_offset, PANEL, 1)
            left_part = lax.dynamic_slice_in_dim(left_strip, row_offset, PANEL, 0)
            next_row = jnp.where(
                active_cols[None, :],
                next_row
                - jnp.dot(
                    left_part, top_strip, precision=HIGHEST, preferred_element_type=jnp.float32
                ),
                next_row,
            )
            next_row = owned_rows(next_row, step_index + 1)
            next_row, next_col = lax.optimization_barrier((next_row, next_col))
            next_col = jnp.where(
                active_rows[:, None],
                next_col
                - jnp.dot(
                    left_strip, top_part, precision=HIGHEST, preferred_element_type=jnp.float32
                ),
                next_col,
            )
            left_next, top_next = share_strips(next_col, next_row, step_index + 1)
        eliminate_matrix = matrix
        eliminate_active_rows, eliminate_active_cols = actives(step_index)
        eliminate_col_owner, eliminate_row_owner, eliminate_col_offset, eliminate_row_offset = (
            strip_bounds(step_index)
        )
        present = lax.dynamic_slice_in_dim(eliminate_matrix, eliminate_col_offset, PANEL, 1)
        fresh_col = jnp.where(
            (col_id == eliminate_col_owner) & eliminate_active_rows[:, None], left_strip, present
        )
        eliminate_matrix = lax.dynamic_update_slice_in_dim(
            eliminate_matrix, fresh_col, eliminate_col_offset, 1
        )
        product = jnp.dot(
            left_strip, top_strip, precision=HIGHEST, preferred_element_type=jnp.float32
        )
        matrix = jnp.where(
            eliminate_active_rows[:, None] & eliminate_active_cols[None, :],
            eliminate_matrix - product,
            eliminate_matrix,
        )
        if step_index + 1 < PANELS:
            left_strip, top_strip = (left_next, top_next)
    return matrix[None]


def solution(mesh):
    placed = (
        P("front", None, "row", "column"),
        P("front", None, None),
        P("front", None, None),
        P("front", None),
        P("front", None),
        P("front", None),
        P("front", None, None, None),
    )
    return jax.shard_map(
        body, mesh=mesh, in_specs=placed, out_specs=P("front", "row", "column"), check_vma=False
    )
```

```python
import jax
import jax.numpy as jnp
from jax import lax
from jax.sharding import PartitionSpec as P
from jax.experimental import pallas as pl
from jax.experimental.pallas import tpu as pltpu

ORDER = 6144
TILE = 128
PANEL = 256
PANELS = 4
ROWMOST = 2


HIGHEST = lax.Precision.HIGHEST


def broadcast(block, axis, source):
    block = jnp.where(lax.axis_index(axis) == source, block, jnp.zeros_like(block))
    return lax.psum(block, axis)


def exchange_broadcast(block, axis, source):
    size = lax.axis_size(axis)
    if size & (size - 1):
        return broadcast(block, axis, source)
    index = lax.axis_index(axis)
    distance = 1
    while distance < size:
        partner = [(i, i ^ distance) for i in range(size)]
        received = lax.ppermute(block, axis, partner)
        take = (source // distance) % 2 != (index // distance) % 2
        block = jnp.where(take, received, block)
        distance *= 2
    return block


def pack_kernel(sources_ref, blocks_ref, out_ref):
    tile_side = out_ref.shape[-1]
    piece_rows = blocks_ref.shape[2] // tile_side
    piece_cols = blocks_ref.shape[3] // tile_side
    per_child = piece_rows * piece_cols

    def place(slot, carry):
        source = sources_ref[slot]

        @pl.when(source >= 0)
        def _():
            child = source // per_child
            row_start = pl.multiple_of((source // piece_cols) % piece_rows * tile_side, tile_side)
            col_start = pl.multiple_of(source % piece_cols * tile_side, tile_side)
            out_ref[slot] = blocks_ref[
                0, child, pl.ds(row_start, tile_side), pl.ds(col_start, tile_side)
            ]

        @pl.when(source < 0)
        def _():
            out_ref[slot] = jnp.zeros((tile_side, tile_side), out_ref.dtype)

        return carry

    lax.fori_loop(0, out_ref.shape[0], place, 0)


def pack_tiles(blocks, target_dev, dest_count, capacity):
    dest_iota = jnp.arange(dest_count, dtype=jnp.int32)
    matches = (target_dev[:, None] == dest_iota[None, :]).astype(jnp.int32)
    earlier = jnp.cumsum(matches, axis=0) - matches
    position = jnp.sum(earlier * matches, axis=1)
    usable = target_dev < dest_count
    slot_index = jnp.where(usable, target_dev * capacity + position, dest_count * capacity)
    tile_ids = jnp.arange(target_dev.shape[0], dtype=jnp.int32)
    sources = (
        jnp.full((dest_count * capacity,), -1, jnp.int32).at[slot_index].set(tile_ids, mode="drop")
    )
    slots = dest_count * capacity
    payload = pl.pallas_call(
        pack_kernel,
        out_shape=jax.ShapeDtypeStruct((slots, TILE, TILE), blocks.dtype),
        grid_spec=pltpu.PrefetchScalarGridSpec(
            num_scalar_prefetch=1,
            grid=(1,),
            in_specs=[pl.BlockSpec(blocks.shape, lambda i, *_: (0, 0, 0, 0))],
            out_specs=pl.BlockSpec((slots, TILE, TILE), lambda i, *_: (0, 0, 0)),
        ),
    )(sources, blocks)
    return payload.reshape((dest_count, capacity, TILE, TILE))


def assemble_kernel(spots_ref, offset_ref, diag_ref, payload_ref, out_ref):
    rows_total, cols_total = out_ref.shape
    tile_side = payload_ref.shape[-1]
    row_tiles = rows_total // tile_side
    col_tiles = cols_total // tile_side
    offset = offset_ref[0]
    for band in range(row_tiles):
        band_rows = pl.ds(band * tile_side, tile_side)
        row_iota = lax.broadcasted_iota(jnp.int32, (tile_side, cols_total), 0) + band * tile_side
        col_iota = lax.broadcasted_iota(jnp.int32, (tile_side, cols_total), 1)
        out_ref[band_rows, :] = jnp.where(
            row_iota + offset == col_iota, diag_ref[band_rows, :], 0.0
        )

    def add_tile(slot, carry):
        spot = spots_ref[slot]
        tile_row = spot // col_tiles
        tile_col = spot % col_tiles

        @pl.when(tile_row < row_tiles)
        def _():
            row_start = pl.multiple_of(tile_row * tile_side, tile_side)
            col_start = pl.multiple_of(tile_col * tile_side, tile_side)
            window = (pl.ds(row_start, tile_side), pl.ds(col_start, tile_side))
            out_ref[window] = out_ref[window] + payload_ref[slot]

        return carry

    lax.fori_loop(0, payload_ref.shape[0], add_tile, 0)


def scatter_tiles(payload, labels, diag_part, offset, local_rows, local_cols):
    tile_side = payload.shape[-1]
    tiles = payload.reshape(-1, tile_side, tile_side)
    slots = tiles.shape[0]
    return pl.pallas_call(
        assemble_kernel,
        out_shape=jax.ShapeDtypeStruct((local_rows, local_cols), jnp.float32),
        grid_spec=pltpu.PrefetchScalarGridSpec(
            num_scalar_prefetch=2,
            grid=(1,),
            in_specs=[
                pl.BlockSpec((local_rows, 1), lambda i, *_: (0, 0)),
                pl.BlockSpec((slots, tile_side, tile_side), lambda i, *_: (0, 0, 0)),
            ],
            out_specs=pl.BlockSpec((local_rows, local_cols), lambda i, *_: (0, 0)),
        ),
    )(labels.reshape(-1), offset.reshape(1), diag_part.reshape(local_rows, 1), tiles)


def arrival_labels(
    row_map, col_map, child_size, groups, row_devs, col_devs, piece_rows, piece_cols,
    row_tiles, col_tiles, sentinel,
):
    children, side = row_map.shape[1], row_map.shape[2]
    span = children * side
    maps = jnp.concatenate(
        [row_map[0].reshape(-1), col_map[0].reshape(-1), child_size[0].reshape(-1)]
    )
    front_id = lax.axis_index("front")
    shifted = [maps] + [
        lax.ppermute(maps, "front", [(i, (i + shift) % groups) for i in range(groups)])
        for shift in range(1, groups)
    ]
    every = jnp.take(
        jnp.stack(shifted), (front_id - jnp.arange(groups, dtype=jnp.int32)) % groups, axis=0
    )
    row_maps = every[:, :span].reshape(groups, children, side)[:, front_id]
    col_maps = every[:, span : 2 * span].reshape(groups, children, side)[:, front_id]
    sizes = every[:, 2 * span :].reshape(groups, children)[:, front_id]
    child_rows = (
        jnp.arange(row_devs, dtype=jnp.int32)[:, None] * piece_rows
        + jnp.arange(piece_rows, dtype=jnp.int32)[None, :]
    )
    child_cols = (
        jnp.arange(col_devs, dtype=jnp.int32)[:, None] * piece_cols
        + jnp.arange(piece_cols, dtype=jnp.int32)[None, :]
    )
    parent_rows = row_maps[:, child_rows]
    parent_cols = col_maps[:, child_cols]
    hit_rows = (child_rows[None] < sizes[:, None, None]) & (
        parent_rows // row_tiles == lax.axis_index("row")
    )
    hit_cols = (child_cols[None] < sizes[:, None, None]) & (
        parent_cols // col_tiles == lax.axis_index("column")
    )
    hit = hit_cols[:, :, None, None, :] & hit_rows[:, None, :, :, None]
    spot = (parent_rows % row_tiles)[:, None, :, :, None] * col_tiles + (
        parent_cols % col_tiles
    )[:, :, None, None, :]
    sources = groups * col_devs * row_devs
    hit = hit.reshape(sources, piece_rows * piece_cols).astype(jnp.int32)
    spot = jnp.broadcast_to(
        spot, (groups, col_devs, row_devs, piece_rows, piece_cols)
    ).reshape(sources, piece_rows * piece_cols)
    rank = jnp.cumsum(hit, axis=1) - hit
    slots = []
    for slot in range(ROWMOST):
        chosen = (hit == 1) & (rank == slot)
        slots.append(
            jnp.where(
                jnp.any(chosen, axis=1), jnp.sum(jnp.where(chosen, spot, 0), axis=1), sentinel
            )
        )
    return jnp.stack(slots, axis=1)


def body(cbs, row_map, col_map, child_size, front_diag, panel_order, pivot_inverse):
    groups = lax.axis_size("front")
    row_devs = lax.axis_size("row")
    col_devs = lax.axis_size("column")
    row_id = lax.axis_index("row")
    col_id = lax.axis_index("column")
    children = cbs.shape[1]
    piece_rows = cbs.shape[2] // TILE
    piece_cols = cbs.shape[3] // TILE
    local_rows = ORDER // row_devs
    local_cols = ORDER // col_devs
    row_tiles = local_rows // TILE
    col_tiles = local_cols // TILE
    sentinel = row_tiles * col_tiles
    child_rows = row_id * piece_rows + jnp.arange(piece_rows, dtype=jnp.int32)
    child_cols = col_id * piece_cols + jnp.arange(piece_cols, dtype=jnp.int32)
    parent_rows = lax.dynamic_slice_in_dim(row_map[0], row_id * piece_rows, piece_rows, 1)
    parent_cols = lax.dynamic_slice_in_dim(col_map[0], col_id * piece_cols, piece_cols, 1)
    live_rows = child_rows[None, :] < child_size[0][:, None]
    live_cols = child_cols[None, :] < child_size[0][:, None]
    owner_rows = parent_rows // row_tiles
    owner_cols = parent_cols // col_tiles
    target_spot = (
        (parent_rows - owner_rows * row_tiles)[:, :, None] * col_tiles
        + (parent_cols - owner_cols * col_tiles)[:, None, :]
    ).reshape(-1)
    usable = (live_rows[:, :, None] & live_cols[:, None, :]).reshape(-1)
    inner_dest = (owner_cols[:, None, :] * row_devs + owner_rows[:, :, None]).reshape(-1)
    all_devices = groups * row_devs * col_devs
    front_ids = jnp.arange(children, dtype=jnp.int32)[:, None]
    whole_dest = (front_ids * (row_devs * col_devs) + inner_dest.reshape(children, -1)).reshape(-1)
    whole_target = jnp.where(usable, whole_dest, all_devices)
    payload = pack_tiles(cbs, whole_target, all_devices, ROWMOST)
    arrived = lax.all_to_all(
        payload, ("front", "column", "row"), split_axis=0, concat_axis=0, tiled=True
    )
    arrived_labels = arrival_labels(
        row_map, col_map, child_size, groups, row_devs, col_devs, piece_rows, piece_cols,
        row_tiles, col_tiles, sentinel,
    )
    row_glob = row_id * local_rows + jnp.arange(local_rows, dtype=jnp.int32)
    col_glob = col_id * local_cols + jnp.arange(local_cols, dtype=jnp.int32)
    diag_part = lax.dynamic_slice_in_dim(front_diag[0], row_id * local_rows, local_rows)
    diag_offset = (row_id * local_rows - col_id * local_cols).astype(jnp.int32)
    matrix = scatter_tiles(arrived, arrived_labels, diag_part, diag_offset, local_rows, local_cols)
    order_row = panel_order[0]
    inverses = pivot_inverse[0]
    panel_rows = local_rows // PANEL
    panel_cols = local_cols // PANEL
    row_block = row_glob // PANEL
    col_block = col_glob // PANEL

    def strip_bounds(step_index):
        pivot_block = order_row[step_index]
        return (
            pivot_block // panel_cols,
            pivot_block // panel_rows,
            pivot_block % panel_cols * PANEL,
            pivot_block % panel_rows * PANEL,
        )

    def actives(step_index):
        chosen = order_row[: step_index + 1]
        active_rows = jnp.all(row_block[:, None] != chosen[None, :], axis=1)
        active_cols = jnp.all(col_block[:, None] != chosen[None, :], axis=1)
        return (active_rows, active_cols)

    def current_strips(matrix, step_index):
        col_owner, row_owner, col_offset, row_offset = strip_bounds(step_index)
        return (
            lax.dynamic_slice_in_dim(matrix, col_offset, PANEL, 1),
            lax.dynamic_slice_in_dim(matrix, row_offset, PANEL, 0),
        )

    def share_strips(col_strip, row_strip, step_index):
        col_owner, row_owner, col_offset, row_offset = strip_bounds(step_index)
        owner_left = jnp.dot(
            col_strip, inverses[step_index], precision=HIGHEST, preferred_element_type=jnp.float32
        )
        left_strip = exchange_broadcast(owner_left, "column", col_owner)
        top_strip = lax.psum(row_strip, "row")
        return (left_strip, top_strip)

    def owned_rows(row_strip, step_index):
        col_owner, row_owner, col_offset, row_offset = strip_bounds(step_index)
        return jnp.where(row_id == row_owner, row_strip, jnp.zeros_like(row_strip))

    first_col, first_row = current_strips(matrix, 0)
    left_strip, top_strip = share_strips(first_col, owned_rows(first_row, 0), 0)
    for step_index in range(PANELS):
        if step_index + 1 < PANELS:
            active_rows, active_cols = actives(step_index)
            next_col, next_row = current_strips(matrix, step_index + 1)
            col_owner, row_owner, col_offset, row_offset = strip_bounds(step_index + 1)
            top_part = lax.dynamic_slice_in_dim(top_strip, col_offset, PANEL, 1)
            left_part = lax.dynamic_slice_in_dim(left_strip, row_offset, PANEL, 0)
            next_row = jnp.where(
                active_cols[None, :],
                next_row
                - jnp.dot(
                    left_part, top_strip, precision=HIGHEST, preferred_element_type=jnp.float32
                ),
                next_row,
            )
            next_row = owned_rows(next_row, step_index + 1)
            next_row, next_col = lax.optimization_barrier((next_row, next_col))
            next_col = jnp.where(
                active_rows[:, None],
                next_col
                - jnp.dot(
                    left_strip, top_part, precision=HIGHEST, preferred_element_type=jnp.float32
                ),
                next_col,
            )
            left_next, top_next = share_strips(next_col, next_row, step_index + 1)
        eliminate_matrix = matrix
        eliminate_active_rows, eliminate_active_cols = actives(step_index)
        product = jnp.dot(
            left_strip, top_strip, precision=HIGHEST, preferred_element_type=jnp.float32
        )
        eliminate_matrix = jnp.where(
            eliminate_active_rows[:, None] & eliminate_active_cols[None, :],
            eliminate_matrix - product,
            eliminate_matrix,
        )
        eliminate_col_owner, eliminate_row_owner, eliminate_col_offset, eliminate_row_offset = (
            strip_bounds(step_index)
        )
        present = lax.dynamic_slice_in_dim(eliminate_matrix, eliminate_col_offset, PANEL, 1)
        fresh_col = jnp.where(
            (col_id == eliminate_col_owner) & eliminate_active_rows[:, None], left_strip, present
        )
        matrix = lax.dynamic_update_slice_in_dim(
            eliminate_matrix, fresh_col, eliminate_col_offset, 1
        )
        if step_index + 1 < PANELS:
            left_strip, top_strip = (left_next, top_next)
    return matrix[None]


def solution(mesh):
    placed = (
        P("front", None, "row", "column"),
        P("front", None, None),
        P("front", None, None),
        P("front", None),
        P("front", None),
        P("front", None),
        P("front", None, None, None),
    )
    return jax.shard_map(
        body, mesh=mesh, in_specs=placed, out_specs=P("front", "row", "column"), check_vma=False
    )
```

```python
import jax
import jax.numpy as jnp
from jax import lax
from jax.sharding import PartitionSpec as P
from jax.experimental import pallas as pl
from jax.experimental.pallas import tpu as pltpu

ORDER = 6144
TILE = 128
PANEL = 256
PANELS = 4
ROWMOST = 2


HIGHEST = lax.Precision.HIGHEST


def broadcast(block, axis, source):
    block = jnp.where(lax.axis_index(axis) == source, block, jnp.zeros_like(block))
    return lax.psum(block, axis)


def exchange_broadcast(block, axis, source):
    size = lax.axis_size(axis)
    if size & (size - 1):
        return broadcast(block, axis, source)
    index = lax.axis_index(axis)
    distance = 1
    while distance < size:
        partner = [(i, i ^ distance) for i in range(size)]
        received = lax.ppermute(block, axis, partner)
        take = (source // distance) % 2 != (index // distance) % 2
        block = jnp.where(take, received, block)
        distance *= 2
    return block


def pack_kernel(sources_ref, blocks_ref, out_ref):
    tile_side = out_ref.shape[-1]
    piece_rows = blocks_ref.shape[2] // tile_side
    piece_cols = blocks_ref.shape[3] // tile_side
    per_child = piece_rows * piece_cols

    def place(slot, carry):
        source = sources_ref[slot]

        @pl.when(source >= 0)
        def _():
            child = source // per_child
            row_start = pl.multiple_of((source // piece_cols) % piece_rows * tile_side, tile_side)
            col_start = pl.multiple_of(source % piece_cols * tile_side, tile_side)
            out_ref[slot] = blocks_ref[
                0, child, pl.ds(row_start, tile_side), pl.ds(col_start, tile_side)
            ]

        @pl.when(source < 0)
        def _():
            out_ref[slot] = jnp.zeros((tile_side, tile_side), out_ref.dtype)

        return carry

    lax.fori_loop(0, out_ref.shape[0], place, 0)


def pack_tiles(blocks, target_dev, dest_count, capacity):
    dest_iota = jnp.arange(dest_count, dtype=jnp.int32)
    matches = (target_dev[:, None] == dest_iota[None, :]).astype(jnp.int32)
    earlier = jnp.cumsum(matches, axis=0) - matches
    position = jnp.sum(earlier * matches, axis=1)
    usable = target_dev < dest_count
    slot_index = jnp.where(usable, target_dev * capacity + position, dest_count * capacity)
    tile_ids = jnp.arange(target_dev.shape[0], dtype=jnp.int32)
    sources = (
        jnp.full((dest_count * capacity,), -1, jnp.int32).at[slot_index].set(tile_ids, mode="drop")
    )
    slots = dest_count * capacity
    payload = pl.pallas_call(
        pack_kernel,
        out_shape=jax.ShapeDtypeStruct((slots, TILE, TILE), blocks.dtype),
        grid_spec=pltpu.PrefetchScalarGridSpec(
            num_scalar_prefetch=1,
            grid=(1,),
            in_specs=[pl.BlockSpec(blocks.shape, lambda i, *_: (0, 0, 0, 0))],
            out_specs=pl.BlockSpec((slots, TILE, TILE), lambda i, *_: (0, 0, 0)),
        ),
    )(sources, blocks)
    return payload.reshape((dest_count, capacity, TILE, TILE))


def assemble_kernel(spots_ref, offset_ref, diag_ref, payload_ref, out_ref):
    rows_total, cols_total = out_ref.shape
    tile_side = payload_ref.shape[-1]
    row_tiles = rows_total // tile_side
    col_tiles = cols_total // tile_side
    offset = offset_ref[0]
    if rows_total == cols_total:
        out_ref[...] = jnp.zeros(out_ref.shape, out_ref.dtype)
        row_iota = lax.broadcasted_iota(jnp.int32, (tile_side, tile_side), 0)
        col_iota = lax.broadcasted_iota(jnp.int32, (tile_side, tile_side), 1)

        @pl.when(offset == 0)
        def _():
            for band in range(row_tiles):
                span = pl.ds(band * tile_side, tile_side)
                out_ref[span, span] = jnp.where(row_iota == col_iota, diag_ref[span, :], 0.0)

    else:
        for band in range(row_tiles):
            band_rows = pl.ds(band * tile_side, tile_side)
            row_iota = lax.broadcasted_iota(jnp.int32, (tile_side, cols_total), 0) + band * tile_side
            col_iota = lax.broadcasted_iota(jnp.int32, (tile_side, cols_total), 1)
            out_ref[band_rows, :] = jnp.where(
                row_iota + offset == col_iota, diag_ref[band_rows, :], 0.0
            )

    def add_tile(slot, carry):
        spot = spots_ref[slot]
        tile_row = spot // col_tiles
        tile_col = spot % col_tiles

        @pl.when(tile_row < row_tiles)
        def _():
            row_start = pl.multiple_of(tile_row * tile_side, tile_side)
            col_start = pl.multiple_of(tile_col * tile_side, tile_side)
            window = (pl.ds(row_start, tile_side), pl.ds(col_start, tile_side))
            out_ref[window] = out_ref[window] + payload_ref[slot]

        return carry

    lax.fori_loop(0, payload_ref.shape[0], add_tile, 0)


def scatter_tiles(payload, labels, diag_part, offset, local_rows, local_cols):
    tile_side = payload.shape[-1]
    tiles = payload.reshape(-1, tile_side, tile_side)
    slots = tiles.shape[0]
    return pl.pallas_call(
        assemble_kernel,
        out_shape=jax.ShapeDtypeStruct((local_rows, local_cols), jnp.float32),
        grid_spec=pltpu.PrefetchScalarGridSpec(
            num_scalar_prefetch=2,
            grid=(1,),
            in_specs=[
                pl.BlockSpec((local_rows, 1), lambda i, *_: (0, 0)),
                pl.BlockSpec((slots, tile_side, tile_side), lambda i, *_: (0, 0, 0)),
            ],
            out_specs=pl.BlockSpec((local_rows, local_cols), lambda i, *_: (0, 0)),
        ),
    )(labels.reshape(-1), offset.reshape(1), diag_part.reshape(local_rows, 1), tiles)


def arrival_labels(
    row_map, col_map, child_size, groups, row_devs, col_devs, piece_rows, piece_cols,
    row_tiles, col_tiles, sentinel,
):
    children, side = row_map.shape[1], row_map.shape[2]
    span = children * side
    maps = jnp.concatenate(
        [row_map[0].reshape(-1), col_map[0].reshape(-1), child_size[0].reshape(-1)]
    )
    every = lax.all_gather(maps, "front")
    front_id = lax.axis_index("front")
    row_maps = every[:, :span].reshape(groups, children, side)[:, front_id]
    col_maps = every[:, span : 2 * span].reshape(groups, children, side)[:, front_id]
    sizes = every[:, 2 * span :].reshape(groups, children)[:, front_id]
    child_rows = (
        jnp.arange(row_devs, dtype=jnp.int32)[:, None] * piece_rows
        + jnp.arange(piece_rows, dtype=jnp.int32)[None, :]
    )
    child_cols = (
        jnp.arange(col_devs, dtype=jnp.int32)[:, None] * piece_cols
        + jnp.arange(piece_cols, dtype=jnp.int32)[None, :]
    )
    parent_rows = row_maps[:, child_rows]
    parent_cols = col_maps[:, child_cols]
    hit_rows = (child_rows[None] < sizes[:, None, None]) & (
        parent_rows // row_tiles == lax.axis_index("row")
    )
    hit_cols = (child_cols[None] < sizes[:, None, None]) & (
        parent_cols // col_tiles == lax.axis_index("column")
    )
    hit = hit_cols[:, :, None, None, :] & hit_rows[:, None, :, :, None]
    spot = (parent_rows % row_tiles)[:, None, :, :, None] * col_tiles + (
        parent_cols % col_tiles
    )[:, :, None, None, :]
    sources = groups * col_devs * row_devs
    hit = hit.reshape(sources, piece_rows * piece_cols).astype(jnp.int32)
    spot = jnp.broadcast_to(
        spot, (groups, col_devs, row_devs, piece_rows, piece_cols)
    ).reshape(sources, piece_rows * piece_cols)
    rank = jnp.cumsum(hit, axis=1) - hit
    slots = []
    for slot in range(ROWMOST):
        chosen = (hit == 1) & (rank == slot)
        slots.append(
            jnp.where(
                jnp.any(chosen, axis=1), jnp.sum(jnp.where(chosen, spot, 0), axis=1), sentinel
            )
        )
    return jnp.stack(slots, axis=1)


def body(cbs, row_map, col_map, child_size, front_diag, panel_order, pivot_inverse):
    groups = lax.axis_size("front")
    row_devs = lax.axis_size("row")
    col_devs = lax.axis_size("column")
    row_id = lax.axis_index("row")
    col_id = lax.axis_index("column")
    children = cbs.shape[1]
    piece_rows = cbs.shape[2] // TILE
    piece_cols = cbs.shape[3] // TILE
    local_rows = ORDER // row_devs
    local_cols = ORDER // col_devs
    row_tiles = local_rows // TILE
    col_tiles = local_cols // TILE
    sentinel = row_tiles * col_tiles
    child_rows = row_id * piece_rows + jnp.arange(piece_rows, dtype=jnp.int32)
    child_cols = col_id * piece_cols + jnp.arange(piece_cols, dtype=jnp.int32)
    parent_rows = lax.dynamic_slice_in_dim(row_map[0], row_id * piece_rows, piece_rows, 1)
    parent_cols = lax.dynamic_slice_in_dim(col_map[0], col_id * piece_cols, piece_cols, 1)
    live_rows = child_rows[None, :] < child_size[0][:, None]
    live_cols = child_cols[None, :] < child_size[0][:, None]
    owner_rows = parent_rows // row_tiles
    owner_cols = parent_cols // col_tiles
    target_spot = (
        (parent_rows - owner_rows * row_tiles)[:, :, None] * col_tiles
        + (parent_cols - owner_cols * col_tiles)[:, None, :]
    ).reshape(-1)
    usable = (live_rows[:, :, None] & live_cols[:, None, :]).reshape(-1)
    inner_dest = (owner_cols[:, None, :] * row_devs + owner_rows[:, :, None]).reshape(-1)
    all_devices = groups * row_devs * col_devs
    front_ids = jnp.arange(children, dtype=jnp.int32)[:, None]
    whole_dest = (front_ids * (row_devs * col_devs) + inner_dest.reshape(children, -1)).reshape(-1)
    whole_target = jnp.where(usable, whole_dest, all_devices)
    payload = pack_tiles(cbs, whole_target, all_devices, ROWMOST)
    arrived = lax.all_to_all(
        payload, ("front", "column", "row"), split_axis=0, concat_axis=0, tiled=True
    )
    arrived_labels = arrival_labels(
        row_map, col_map, child_size, groups, row_devs, col_devs, piece_rows, piece_cols,
        row_tiles, col_tiles, sentinel,
    )
    row_glob = row_id * local_rows + jnp.arange(local_rows, dtype=jnp.int32)
    col_glob = col_id * local_cols + jnp.arange(local_cols, dtype=jnp.int32)
    diag_part = lax.dynamic_slice_in_dim(front_diag[0], row_id * local_rows, local_rows)
    diag_offset = (row_id * local_rows - col_id * local_cols).astype(jnp.int32)
    matrix = scatter_tiles(arrived, arrived_labels, diag_part, diag_offset, local_rows, local_cols)
    order_row = panel_order[0]
    inverses = pivot_inverse[0]
    panel_rows = local_rows // PANEL
    panel_cols = local_cols // PANEL
    row_block = row_glob // PANEL
    col_block = col_glob // PANEL

    def strip_bounds(step_index):
        pivot_block = order_row[step_index]
        return (
            pivot_block // panel_cols,
            pivot_block // panel_rows,
            pivot_block % panel_cols * PANEL,
            pivot_block % panel_rows * PANEL,
        )

    def actives(step_index):
        chosen = order_row[: step_index + 1]
        active_rows = jnp.all(row_block[:, None] != chosen[None, :], axis=1)
        active_cols = jnp.all(col_block[:, None] != chosen[None, :], axis=1)
        return (active_rows, active_cols)

    def current_strips(matrix, step_index):
        col_owner, row_owner, col_offset, row_offset = strip_bounds(step_index)
        return (
            lax.dynamic_slice_in_dim(matrix, col_offset, PANEL, 1),
            lax.dynamic_slice_in_dim(matrix, row_offset, PANEL, 0),
        )

    def share_strips(col_strip, row_strip, step_index):
        col_owner, row_owner, col_offset, row_offset = strip_bounds(step_index)
        owner_left = jnp.dot(
            col_strip, inverses[step_index], precision=HIGHEST, preferred_element_type=jnp.float32
        )
        left_strip = exchange_broadcast(owner_left, "column", col_owner)
        top_strip = lax.psum(row_strip, "row")
        return (left_strip, top_strip)

    def owned_rows(row_strip, step_index):
        col_owner, row_owner, col_offset, row_offset = strip_bounds(step_index)
        return jnp.where(row_id == row_owner, row_strip, jnp.zeros_like(row_strip))

    first_col, first_row = current_strips(matrix, 0)
    left_strip, top_strip = share_strips(first_col, owned_rows(first_row, 0), 0)
    for step_index in range(PANELS):
        if step_index + 1 < PANELS:
            active_rows, active_cols = actives(step_index)
            next_col, next_row = current_strips(matrix, step_index + 1)
            col_owner, row_owner, col_offset, row_offset = strip_bounds(step_index + 1)
            top_part = lax.dynamic_slice_in_dim(top_strip, col_offset, PANEL, 1)
            left_part = lax.dynamic_slice_in_dim(left_strip, row_offset, PANEL, 0)
            next_row = jnp.where(
                active_cols[None, :],
                next_row
                - jnp.dot(
                    left_part, top_strip, precision=HIGHEST, preferred_element_type=jnp.float32
                ),
                next_row,
            )
            next_row = owned_rows(next_row, step_index + 1)
            next_row, next_col = lax.optimization_barrier((next_row, next_col))
            next_col = jnp.where(
                active_rows[:, None],
                next_col
                - jnp.dot(
                    left_strip, top_part, precision=HIGHEST, preferred_element_type=jnp.float32
                ),
                next_col,
            )
            left_next, top_next = share_strips(next_col, next_row, step_index + 1)
        eliminate_matrix = matrix
        eliminate_active_rows, eliminate_active_cols = actives(step_index)
        product = jnp.dot(
            left_strip, top_strip, precision=HIGHEST, preferred_element_type=jnp.float32
        )
        eliminate_matrix = jnp.where(
            eliminate_active_rows[:, None] & eliminate_active_cols[None, :],
            eliminate_matrix - product,
            eliminate_matrix,
        )
        eliminate_col_owner, eliminate_row_owner, eliminate_col_offset, eliminate_row_offset = (
            strip_bounds(step_index)
        )
        present = lax.dynamic_slice_in_dim(eliminate_matrix, eliminate_col_offset, PANEL, 1)
        fresh_col = jnp.where(
            (col_id == eliminate_col_owner) & eliminate_active_rows[:, None], left_strip, present
        )
        matrix = lax.dynamic_update_slice_in_dim(
            eliminate_matrix, fresh_col, eliminate_col_offset, 1
        )
        if step_index + 1 < PANELS:
            left_strip, top_strip = (left_next, top_next)
    return matrix[None]


def solution(mesh):
    placed = (
        P("front", None, "row", "column"),
        P("front", None, None),
        P("front", None, None),
        P("front", None),
        P("front", None),
        P("front", None),
        P("front", None, None, None),
    )
    return jax.shard_map(
        body, mesh=mesh, in_specs=placed, out_specs=P("front", "row", "column"), check_vma=False
    )
```

```python
import jax
import jax.numpy as jnp
from jax import lax
from jax.sharding import PartitionSpec as P
from jax.experimental import pallas as pl
from jax.experimental.pallas import tpu as pltpu

ORDER = 6144
TILE = 128
PANEL = 256
PANELS = 4
ROWMOST = 2


HIGHEST = lax.Precision.HIGHEST


def broadcast(block, axis, source):
    block = jnp.where(lax.axis_index(axis) == source, block, jnp.zeros_like(block))
    return lax.psum(block, axis)


def exchange_broadcast(block, axis, source):
    size = lax.axis_size(axis)
    if size & (size - 1):
        return broadcast(block, axis, source)
    index = lax.axis_index(axis)
    distance = 1
    while distance < size:
        partner = [(i, i ^ distance) for i in range(size)]
        received = lax.ppermute(block, axis, partner)
        take = (source // distance) % 2 != (index // distance) % 2
        block = jnp.where(take, received, block)
        distance *= 2
    return block


def pack_kernel(sources_ref, blocks_ref, out_ref):
    tile_side = out_ref.shape[-1]
    piece_rows = blocks_ref.shape[2] // tile_side
    piece_cols = blocks_ref.shape[3] // tile_side
    per_child = piece_rows * piece_cols

    def place(slot, carry):
        source = sources_ref[slot]

        @pl.when(source >= 0)
        def _():
            child = source // per_child
            row_start = pl.multiple_of((source // piece_cols) % piece_rows * tile_side, tile_side)
            col_start = pl.multiple_of(source % piece_cols * tile_side, tile_side)
            out_ref[slot] = blocks_ref[
                0, child, pl.ds(row_start, tile_side), pl.ds(col_start, tile_side)
            ]

        return carry

    lax.fori_loop(0, out_ref.shape[0], place, 0)


def pack_tiles(blocks, target_dev, dest_count, capacity):
    dest_iota = jnp.arange(dest_count, dtype=jnp.int32)
    matches = (target_dev[:, None] == dest_iota[None, :]).astype(jnp.int32)
    earlier = jnp.cumsum(matches, axis=0) - matches
    position = jnp.sum(earlier * matches, axis=1)
    usable = target_dev < dest_count
    slot_index = jnp.where(usable, target_dev * capacity + position, dest_count * capacity)
    tile_ids = jnp.arange(target_dev.shape[0], dtype=jnp.int32)
    sources = (
        jnp.full((dest_count * capacity,), -1, jnp.int32).at[slot_index].set(tile_ids, mode="drop")
    )
    slots = dest_count * capacity
    payload = pl.pallas_call(
        pack_kernel,
        out_shape=jax.ShapeDtypeStruct((slots, TILE, TILE), blocks.dtype),
        grid_spec=pltpu.PrefetchScalarGridSpec(
            num_scalar_prefetch=1,
            grid=(1,),
            in_specs=[pl.BlockSpec(blocks.shape, lambda i, *_: (0, 0, 0, 0))],
            out_specs=pl.BlockSpec((slots, TILE, TILE), lambda i, *_: (0, 0, 0)),
        ),
    )(sources, blocks)
    return payload.reshape((dest_count, capacity, TILE, TILE))


def assemble_kernel(spots_ref, offset_ref, diag_ref, payload_ref, out_ref):
    rows_total, cols_total = out_ref.shape
    tile_side = payload_ref.shape[-1]
    row_tiles = rows_total // tile_side
    col_tiles = cols_total // tile_side
    offset = offset_ref[0]
    if rows_total == cols_total:
        out_ref[...] = jnp.zeros(out_ref.shape, out_ref.dtype)
        row_iota = lax.broadcasted_iota(jnp.int32, (tile_side, tile_side), 0)
        col_iota = lax.broadcasted_iota(jnp.int32, (tile_side, tile_side), 1)

        @pl.when(offset == 0)
        def _():
            for band in range(row_tiles):
                span = pl.ds(band * tile_side, tile_side)
                out_ref[span, span] = jnp.where(row_iota == col_iota, diag_ref[span, :], 0.0)

    else:
        for band in range(row_tiles):
            band_rows = pl.ds(band * tile_side, tile_side)
            row_iota = lax.broadcasted_iota(jnp.int32, (tile_side, cols_total), 0) + band * tile_side
            col_iota = lax.broadcasted_iota(jnp.int32, (tile_side, cols_total), 1)
            out_ref[band_rows, :] = jnp.where(
                row_iota + offset == col_iota, diag_ref[band_rows, :], 0.0
            )

    def add_tile(slot, carry):
        spot = spots_ref[slot]
        tile_row = spot // col_tiles
        tile_col = spot % col_tiles

        @pl.when(tile_row < row_tiles)
        def _():
            row_start = pl.multiple_of(tile_row * tile_side, tile_side)
            col_start = pl.multiple_of(tile_col * tile_side, tile_side)
            window = (pl.ds(row_start, tile_side), pl.ds(col_start, tile_side))
            out_ref[window] = out_ref[window] + payload_ref[slot]

        return carry

    lax.fori_loop(0, payload_ref.shape[0], add_tile, 0)


def scatter_tiles(payload, labels, diag_part, offset, local_rows, local_cols):
    tile_side = payload.shape[-1]
    tiles = payload.reshape(-1, tile_side, tile_side)
    slots = tiles.shape[0]
    return pl.pallas_call(
        assemble_kernel,
        out_shape=jax.ShapeDtypeStruct((local_rows, local_cols), jnp.float32),
        grid_spec=pltpu.PrefetchScalarGridSpec(
            num_scalar_prefetch=2,
            grid=(1,),
            in_specs=[
                pl.BlockSpec((local_rows, 1), lambda i, *_: (0, 0)),
                pl.BlockSpec((slots, tile_side, tile_side), lambda i, *_: (0, 0, 0)),
            ],
            out_specs=pl.BlockSpec((local_rows, local_cols), lambda i, *_: (0, 0)),
        ),
    )(labels.reshape(-1), offset.reshape(1), diag_part.reshape(local_rows, 1), tiles)


def arrival_labels(
    row_map, col_map, child_size, groups, row_devs, col_devs, piece_rows, piece_cols,
    row_tiles, col_tiles, sentinel,
):
    children, side = row_map.shape[1], row_map.shape[2]
    span = children * side
    maps = jnp.concatenate(
        [row_map[0].reshape(-1), col_map[0].reshape(-1), child_size[0].reshape(-1)]
    )
    every = lax.all_gather(maps, "front")
    front_id = lax.axis_index("front")
    row_maps = every[:, :span].reshape(groups, children, side)[:, front_id]
    col_maps = every[:, span : 2 * span].reshape(groups, children, side)[:, front_id]
    sizes = every[:, 2 * span :].reshape(groups, children)[:, front_id]
    child_rows = (
        jnp.arange(row_devs, dtype=jnp.int32)[:, None] * piece_rows
        + jnp.arange(piece_rows, dtype=jnp.int32)[None, :]
    )
    child_cols = (
        jnp.arange(col_devs, dtype=jnp.int32)[:, None] * piece_cols
        + jnp.arange(piece_cols, dtype=jnp.int32)[None, :]
    )
    parent_rows = row_maps[:, child_rows]
    parent_cols = col_maps[:, child_cols]
    hit_rows = (child_rows[None] < sizes[:, None, None]) & (
        parent_rows // row_tiles == lax.axis_index("row")
    )
    hit_cols = (child_cols[None] < sizes[:, None, None]) & (
        parent_cols // col_tiles == lax.axis_index("column")
    )
    hit = hit_cols[:, :, None, None, :] & hit_rows[:, None, :, :, None]
    spot = (parent_rows % row_tiles)[:, None, :, :, None] * col_tiles + (
        parent_cols % col_tiles
    )[:, :, None, None, :]
    sources = groups * col_devs * row_devs
    hit = hit.reshape(sources, piece_rows * piece_cols).astype(jnp.int32)
    spot = jnp.broadcast_to(
        spot, (groups, col_devs, row_devs, piece_rows, piece_cols)
    ).reshape(sources, piece_rows * piece_cols)
    rank = jnp.cumsum(hit, axis=1) - hit
    slots = []
    for slot in range(ROWMOST):
        chosen = (hit == 1) & (rank == slot)
        slots.append(
            jnp.where(
                jnp.any(chosen, axis=1), jnp.sum(jnp.where(chosen, spot, 0), axis=1), sentinel
            )
        )
    return jnp.stack(slots, axis=1)


def body(cbs, row_map, col_map, child_size, front_diag, panel_order, pivot_inverse):
    groups = lax.axis_size("front")
    row_devs = lax.axis_size("row")
    col_devs = lax.axis_size("column")
    row_id = lax.axis_index("row")
    col_id = lax.axis_index("column")
    children = cbs.shape[1]
    piece_rows = cbs.shape[2] // TILE
    piece_cols = cbs.shape[3] // TILE
    local_rows = ORDER // row_devs
    local_cols = ORDER // col_devs
    row_tiles = local_rows // TILE
    col_tiles = local_cols // TILE
    sentinel = row_tiles * col_tiles
    child_rows = row_id * piece_rows + jnp.arange(piece_rows, dtype=jnp.int32)
    child_cols = col_id * piece_cols + jnp.arange(piece_cols, dtype=jnp.int32)
    parent_rows = lax.dynamic_slice_in_dim(row_map[0], row_id * piece_rows, piece_rows, 1)
    parent_cols = lax.dynamic_slice_in_dim(col_map[0], col_id * piece_cols, piece_cols, 1)
    live_rows = child_rows[None, :] < child_size[0][:, None]
    live_cols = child_cols[None, :] < child_size[0][:, None]
    owner_rows = parent_rows // row_tiles
    owner_cols = parent_cols // col_tiles
    target_spot = (
        (parent_rows - owner_rows * row_tiles)[:, :, None] * col_tiles
        + (parent_cols - owner_cols * col_tiles)[:, None, :]
    ).reshape(-1)
    usable = (live_rows[:, :, None] & live_cols[:, None, :]).reshape(-1)
    inner_dest = (owner_cols[:, None, :] * row_devs + owner_rows[:, :, None]).reshape(-1)
    all_devices = groups * row_devs * col_devs
    front_ids = jnp.arange(children, dtype=jnp.int32)[:, None]
    whole_dest = (front_ids * (row_devs * col_devs) + inner_dest.reshape(children, -1)).reshape(-1)
    whole_target = jnp.where(usable, whole_dest, all_devices)
    payload = pack_tiles(cbs, whole_target, all_devices, ROWMOST)
    arrived = lax.all_to_all(
        payload, ("front", "column", "row"), split_axis=0, concat_axis=0, tiled=True
    )
    arrived_labels = arrival_labels(
        row_map, col_map, child_size, groups, row_devs, col_devs, piece_rows, piece_cols,
        row_tiles, col_tiles, sentinel,
    )
    row_glob = row_id * local_rows + jnp.arange(local_rows, dtype=jnp.int32)
    col_glob = col_id * local_cols + jnp.arange(local_cols, dtype=jnp.int32)
    diag_part = lax.dynamic_slice_in_dim(front_diag[0], row_id * local_rows, local_rows)
    diag_offset = (row_id * local_rows - col_id * local_cols).astype(jnp.int32)
    matrix = scatter_tiles(arrived, arrived_labels, diag_part, diag_offset, local_rows, local_cols)
    order_row = panel_order[0]
    inverses = pivot_inverse[0]
    panel_rows = local_rows // PANEL
    panel_cols = local_cols // PANEL
    row_block = row_glob // PANEL
    col_block = col_glob // PANEL

    def strip_bounds(step_index):
        pivot_block = order_row[step_index]
        return (
            pivot_block // panel_cols,
            pivot_block // panel_rows,
            pivot_block % panel_cols * PANEL,
            pivot_block % panel_rows * PANEL,
        )

    def actives(step_index):
        chosen = order_row[: step_index + 1]
        active_rows = jnp.all(row_block[:, None] != chosen[None, :], axis=1)
        active_cols = jnp.all(col_block[:, None] != chosen[None, :], axis=1)
        return (active_rows, active_cols)

    def current_strips(matrix, step_index):
        col_owner, row_owner, col_offset, row_offset = strip_bounds(step_index)
        return (
            lax.dynamic_slice_in_dim(matrix, col_offset, PANEL, 1),
            lax.dynamic_slice_in_dim(matrix, row_offset, PANEL, 0),
        )

    def share_strips(col_strip, row_strip, step_index):
        col_owner, row_owner, col_offset, row_offset = strip_bounds(step_index)
        owner_left = jnp.dot(
            col_strip, inverses[step_index], precision=HIGHEST, preferred_element_type=jnp.float32
        )
        left_strip = exchange_broadcast(owner_left, "column", col_owner)
        top_strip = lax.psum(row_strip, "row")
        return (left_strip, top_strip)

    def owned_rows(row_strip, step_index):
        col_owner, row_owner, col_offset, row_offset = strip_bounds(step_index)
        return jnp.where(row_id == row_owner, row_strip, jnp.zeros_like(row_strip))

    first_col, first_row = current_strips(matrix, 0)
    left_strip, top_strip = share_strips(first_col, owned_rows(first_row, 0), 0)
    for step_index in range(PANELS):
        if step_index + 1 < PANELS:
            active_rows, active_cols = actives(step_index)
            next_col, next_row = current_strips(matrix, step_index + 1)
            col_owner, row_owner, col_offset, row_offset = strip_bounds(step_index + 1)
            top_part = lax.dynamic_slice_in_dim(top_strip, col_offset, PANEL, 1)
            left_part = lax.dynamic_slice_in_dim(left_strip, row_offset, PANEL, 0)
            next_row = jnp.where(
                active_cols[None, :],
                next_row
                - jnp.dot(
                    left_part, top_strip, precision=HIGHEST, preferred_element_type=jnp.float32
                ),
                next_row,
            )
            next_row = owned_rows(next_row, step_index + 1)
            next_row, next_col = lax.optimization_barrier((next_row, next_col))
            next_col = jnp.where(
                active_rows[:, None],
                next_col
                - jnp.dot(
                    left_strip, top_part, precision=HIGHEST, preferred_element_type=jnp.float32
                ),
                next_col,
            )
            left_next, top_next = share_strips(next_col, next_row, step_index + 1)
        eliminate_matrix = matrix
        eliminate_active_rows, eliminate_active_cols = actives(step_index)
        product = jnp.dot(
            left_strip, top_strip, precision=HIGHEST, preferred_element_type=jnp.float32
        )
        eliminate_matrix = jnp.where(
            eliminate_active_rows[:, None] & eliminate_active_cols[None, :],
            eliminate_matrix - product,
            eliminate_matrix,
        )
        eliminate_col_owner, eliminate_row_owner, eliminate_col_offset, eliminate_row_offset = (
            strip_bounds(step_index)
        )
        present = lax.dynamic_slice_in_dim(eliminate_matrix, eliminate_col_offset, PANEL, 1)
        fresh_col = jnp.where(
            (col_id == eliminate_col_owner) & eliminate_active_rows[:, None], left_strip, present
        )
        matrix = lax.dynamic_update_slice_in_dim(
            eliminate_matrix, fresh_col, eliminate_col_offset, 1
        )
        if step_index + 1 < PANELS:
            left_strip, top_strip = (left_next, top_next)
    return matrix[None]


def solution(mesh):
    placed = (
        P("front", None, "row", "column"),
        P("front", None, None),
        P("front", None, None),
        P("front", None),
        P("front", None),
        P("front", None),
        P("front", None, None, None),
    )
    return jax.shard_map(
        body, mesh=mesh, in_specs=placed, out_specs=P("front", "row", "column"), check_vma=False
    )
```

```python
import jax
import jax.numpy as jnp
from jax import lax
from jax.sharding import PartitionSpec as P
from jax.experimental import pallas as pl
from jax.experimental.pallas import tpu as pltpu

ORDER = 6144
TILE = 128
PANEL = 256
PANELS = 4
ROWMOST = 2


HIGHEST = lax.Precision.HIGHEST


def broadcast(block, axis, source):
    block = jnp.where(lax.axis_index(axis) == source, block, jnp.zeros_like(block))
    return lax.psum(block, axis)


def exchange_broadcast(block, axis, source):
    size = lax.axis_size(axis)
    if size & (size - 1):
        return broadcast(block, axis, source)
    index = lax.axis_index(axis)
    distance = 1
    while distance < size:
        partner = [(i, i ^ distance) for i in range(size)]
        received = lax.ppermute(block, axis, partner)
        take = (source // distance) % 2 != (index // distance) % 2
        block = jnp.where(take, received, block)
        distance *= 2
    return block


def pack_kernel(sources_ref, blocks_ref, out_ref):
    tile_side = out_ref.shape[-1]
    piece_rows = blocks_ref.shape[2] // tile_side
    piece_cols = blocks_ref.shape[3] // tile_side
    per_child = piece_rows * piece_cols

    def place(slot, carry):
        source = sources_ref[slot]

        @pl.when(source >= 0)
        def _():
            child = source // per_child
            row_start = pl.multiple_of((source // piece_cols) % piece_rows * tile_side, tile_side)
            col_start = pl.multiple_of(source % piece_cols * tile_side, tile_side)
            out_ref[slot] = blocks_ref[
                0, child, pl.ds(row_start, tile_side), pl.ds(col_start, tile_side)
            ]

        return carry

    lax.fori_loop(0, out_ref.shape[0], place, 0, unroll=8)


def pack_tiles(blocks, target_dev, dest_count, capacity):
    dest_iota = jnp.arange(dest_count, dtype=jnp.int32)
    matches = (target_dev[:, None] == dest_iota[None, :]).astype(jnp.int32)
    earlier = jnp.cumsum(matches, axis=0) - matches
    position = jnp.sum(earlier * matches, axis=1)
    usable = target_dev < dest_count
    slot_index = jnp.where(usable, target_dev * capacity + position, dest_count * capacity)
    tile_ids = jnp.arange(target_dev.shape[0], dtype=jnp.int32)
    sources = (
        jnp.full((dest_count * capacity,), -1, jnp.int32).at[slot_index].set(tile_ids, mode="drop")
    )
    slots = dest_count * capacity
    payload = pl.pallas_call(
        pack_kernel,
        out_shape=jax.ShapeDtypeStruct((slots, TILE, TILE), blocks.dtype),
        grid_spec=pltpu.PrefetchScalarGridSpec(
            num_scalar_prefetch=1,
            grid=(1,),
            in_specs=[pl.BlockSpec(blocks.shape, lambda i, *_: (0, 0, 0, 0))],
            out_specs=pl.BlockSpec((slots, TILE, TILE), lambda i, *_: (0, 0, 0)),
        ),
    )(sources, blocks)
    return payload.reshape((dest_count, capacity, TILE, TILE))


def assemble_kernel(spots_ref, offset_ref, diag_ref, payload_ref, out_ref):
    rows_total, cols_total = out_ref.shape
    tile_side = payload_ref.shape[-1]
    row_tiles = rows_total // tile_side
    col_tiles = cols_total // tile_side
    offset = offset_ref[0]
    if rows_total == cols_total:
        out_ref[...] = jnp.zeros(out_ref.shape, out_ref.dtype)
        row_iota = lax.broadcasted_iota(jnp.int32, (tile_side, tile_side), 0)
        col_iota = lax.broadcasted_iota(jnp.int32, (tile_side, tile_side), 1)

        @pl.when(offset == 0)
        def _():
            for band in range(row_tiles):
                span = pl.ds(band * tile_side, tile_side)
                out_ref[span, span] = jnp.where(row_iota == col_iota, diag_ref[span, :], 0.0)

    else:
        for band in range(row_tiles):
            band_rows = pl.ds(band * tile_side, tile_side)
            row_iota = lax.broadcasted_iota(jnp.int32, (tile_side, cols_total), 0) + band * tile_side
            col_iota = lax.broadcasted_iota(jnp.int32, (tile_side, cols_total), 1)
            out_ref[band_rows, :] = jnp.where(
                row_iota + offset == col_iota, diag_ref[band_rows, :], 0.0
            )

    def add_tile(slot, carry):
        spot = spots_ref[slot]
        tile_row = spot // col_tiles
        tile_col = spot % col_tiles

        @pl.when(tile_row < row_tiles)
        def _():
            row_start = pl.multiple_of(tile_row * tile_side, tile_side)
            col_start = pl.multiple_of(tile_col * tile_side, tile_side)
            window = (pl.ds(row_start, tile_side), pl.ds(col_start, tile_side))
            out_ref[window] = out_ref[window] + payload_ref[slot]

        return carry

    lax.fori_loop(0, payload_ref.shape[0], add_tile, 0, unroll=8)


def scatter_tiles(payload, labels, diag_part, offset, local_rows, local_cols):
    tile_side = payload.shape[-1]
    tiles = payload.reshape(-1, tile_side, tile_side)
    slots = tiles.shape[0]
    return pl.pallas_call(
        assemble_kernel,
        out_shape=jax.ShapeDtypeStruct((local_rows, local_cols), jnp.float32),
        grid_spec=pltpu.PrefetchScalarGridSpec(
            num_scalar_prefetch=2,
            grid=(1,),
            in_specs=[
                pl.BlockSpec((local_rows, 1), lambda i, *_: (0, 0)),
                pl.BlockSpec((slots, tile_side, tile_side), lambda i, *_: (0, 0, 0)),
            ],
            out_specs=pl.BlockSpec((local_rows, local_cols), lambda i, *_: (0, 0)),
        ),
    )(labels.reshape(-1), offset.reshape(1), diag_part.reshape(local_rows, 1), tiles)


def arrival_labels(
    row_map, col_map, child_size, groups, row_devs, col_devs, piece_rows, piece_cols,
    row_tiles, col_tiles, sentinel,
):
    children, side = row_map.shape[1], row_map.shape[2]
    span = children * side
    maps = jnp.concatenate(
        [row_map[0].reshape(-1), col_map[0].reshape(-1), child_size[0].reshape(-1)]
    )
    every = lax.all_gather(maps, "front")
    front_id = lax.axis_index("front")
    row_maps = every[:, :span].reshape(groups, children, side)[:, front_id]
    col_maps = every[:, span : 2 * span].reshape(groups, children, side)[:, front_id]
    sizes = every[:, 2 * span :].reshape(groups, children)[:, front_id]
    child_rows = (
        jnp.arange(row_devs, dtype=jnp.int32)[:, None] * piece_rows
        + jnp.arange(piece_rows, dtype=jnp.int32)[None, :]
    )
    child_cols = (
        jnp.arange(col_devs, dtype=jnp.int32)[:, None] * piece_cols
        + jnp.arange(piece_cols, dtype=jnp.int32)[None, :]
    )
    parent_rows = row_maps[:, child_rows]
    parent_cols = col_maps[:, child_cols]
    hit_rows = (child_rows[None] < sizes[:, None, None]) & (
        parent_rows // row_tiles == lax.axis_index("row")
    )
    hit_cols = (child_cols[None] < sizes[:, None, None]) & (
        parent_cols // col_tiles == lax.axis_index("column")
    )
    hit = hit_cols[:, :, None, None, :] & hit_rows[:, None, :, :, None]
    spot = (parent_rows % row_tiles)[:, None, :, :, None] * col_tiles + (
        parent_cols % col_tiles
    )[:, :, None, None, :]
    sources = groups * col_devs * row_devs
    hit = hit.reshape(sources, piece_rows * piece_cols).astype(jnp.int32)
    spot = jnp.broadcast_to(
        spot, (groups, col_devs, row_devs, piece_rows, piece_cols)
    ).reshape(sources, piece_rows * piece_cols)
    rank = jnp.cumsum(hit, axis=1) - hit
    slots = []
    for slot in range(ROWMOST):
        chosen = (hit == 1) & (rank == slot)
        slots.append(
            jnp.where(
                jnp.any(chosen, axis=1), jnp.sum(jnp.where(chosen, spot, 0), axis=1), sentinel
            )
        )
    return jnp.stack(slots, axis=1)


def body(cbs, row_map, col_map, child_size, front_diag, panel_order, pivot_inverse):
    groups = lax.axis_size("front")
    row_devs = lax.axis_size("row")
    col_devs = lax.axis_size("column")
    row_id = lax.axis_index("row")
    col_id = lax.axis_index("column")
    children = cbs.shape[1]
    piece_rows = cbs.shape[2] // TILE
    piece_cols = cbs.shape[3] // TILE
    local_rows = ORDER // row_devs
    local_cols = ORDER // col_devs
    row_tiles = local_rows // TILE
    col_tiles = local_cols // TILE
    sentinel = row_tiles * col_tiles
    child_rows = row_id * piece_rows + jnp.arange(piece_rows, dtype=jnp.int32)
    child_cols = col_id * piece_cols + jnp.arange(piece_cols, dtype=jnp.int32)
    parent_rows = lax.dynamic_slice_in_dim(row_map[0], row_id * piece_rows, piece_rows, 1)
    parent_cols = lax.dynamic_slice_in_dim(col_map[0], col_id * piece_cols, piece_cols, 1)
    live_rows = child_rows[None, :] < child_size[0][:, None]
    live_cols = child_cols[None, :] < child_size[0][:, None]
    owner_rows = parent_rows // row_tiles
    owner_cols = parent_cols // col_tiles
    target_spot = (
        (parent_rows - owner_rows * row_tiles)[:, :, None] * col_tiles
        + (parent_cols - owner_cols * col_tiles)[:, None, :]
    ).reshape(-1)
    usable = (live_rows[:, :, None] & live_cols[:, None, :]).reshape(-1)
    inner_dest = (owner_cols[:, None, :] * row_devs + owner_rows[:, :, None]).reshape(-1)
    all_devices = groups * row_devs * col_devs
    front_ids = jnp.arange(children, dtype=jnp.int32)[:, None]
    whole_dest = (front_ids * (row_devs * col_devs) + inner_dest.reshape(children, -1)).reshape(-1)
    whole_target = jnp.where(usable, whole_dest, all_devices)
    payload = pack_tiles(cbs, whole_target, all_devices, ROWMOST)
    arrived = lax.all_to_all(
        payload, ("front", "column", "row"), split_axis=0, concat_axis=0, tiled=True
    )
    arrived_labels = arrival_labels(
        row_map, col_map, child_size, groups, row_devs, col_devs, piece_rows, piece_cols,
        row_tiles, col_tiles, sentinel,
    )
    row_glob = row_id * local_rows + jnp.arange(local_rows, dtype=jnp.int32)
    col_glob = col_id * local_cols + jnp.arange(local_cols, dtype=jnp.int32)
    diag_part = lax.dynamic_slice_in_dim(front_diag[0], row_id * local_rows, local_rows)
    diag_offset = (row_id * local_rows - col_id * local_cols).astype(jnp.int32)
    matrix = scatter_tiles(arrived, arrived_labels, diag_part, diag_offset, local_rows, local_cols)
    order_row = panel_order[0]
    inverses = pivot_inverse[0]
    panel_rows = local_rows // PANEL
    panel_cols = local_cols // PANEL
    row_block = row_glob // PANEL
    col_block = col_glob // PANEL

    def strip_bounds(step_index):
        pivot_block = order_row[step_index]
        return (
            pivot_block // panel_cols,
            pivot_block // panel_rows,
            pivot_block % panel_cols * PANEL,
            pivot_block % panel_rows * PANEL,
        )

    def actives(step_index):
        chosen = order_row[: step_index + 1]
        active_rows = jnp.all(row_block[:, None] != chosen[None, :], axis=1)
        active_cols = jnp.all(col_block[:, None] != chosen[None, :], axis=1)
        return (active_rows, active_cols)

    def current_strips(matrix, step_index):
        col_owner, row_owner, col_offset, row_offset = strip_bounds(step_index)
        return (
            lax.dynamic_slice_in_dim(matrix, col_offset, PANEL, 1),
            lax.dynamic_slice_in_dim(matrix, row_offset, PANEL, 0),
        )

    def share_strips(col_strip, row_strip, step_index):
        col_owner, row_owner, col_offset, row_offset = strip_bounds(step_index)
        owner_left = jnp.dot(
            col_strip, inverses[step_index], precision=HIGHEST, preferred_element_type=jnp.float32
        )
        left_strip = exchange_broadcast(owner_left, "column", col_owner)
        top_strip = lax.psum(row_strip, "row")
        return (left_strip, top_strip)

    def owned_rows(row_strip, step_index):
        col_owner, row_owner, col_offset, row_offset = strip_bounds(step_index)
        return jnp.where(row_id == row_owner, row_strip, jnp.zeros_like(row_strip))

    first_col, first_row = current_strips(matrix, 0)
    left_strip, top_strip = share_strips(first_col, owned_rows(first_row, 0), 0)
    for step_index in range(PANELS):
        if step_index + 1 < PANELS:
            active_rows, active_cols = actives(step_index)
            next_col, next_row = current_strips(matrix, step_index + 1)
            col_owner, row_owner, col_offset, row_offset = strip_bounds(step_index + 1)
            top_part = lax.dynamic_slice_in_dim(top_strip, col_offset, PANEL, 1)
            left_part = lax.dynamic_slice_in_dim(left_strip, row_offset, PANEL, 0)
            next_row = jnp.where(
                active_cols[None, :],
                next_row
                - jnp.dot(
                    left_part, top_strip, precision=HIGHEST, preferred_element_type=jnp.float32
                ),
                next_row,
            )
            next_row = owned_rows(next_row, step_index + 1)
            next_row, next_col = lax.optimization_barrier((next_row, next_col))
            next_col = jnp.where(
                active_rows[:, None],
                next_col
                - jnp.dot(
                    left_strip, top_part, precision=HIGHEST, preferred_element_type=jnp.float32
                ),
                next_col,
            )
            left_next, top_next = share_strips(next_col, next_row, step_index + 1)
        eliminate_matrix = matrix
        eliminate_active_rows, eliminate_active_cols = actives(step_index)
        product = jnp.dot(
            left_strip, top_strip, precision=HIGHEST, preferred_element_type=jnp.float32
        )
        eliminate_matrix = jnp.where(
            eliminate_active_rows[:, None] & eliminate_active_cols[None, :],
            eliminate_matrix - product,
            eliminate_matrix,
        )
        eliminate_col_owner, eliminate_row_owner, eliminate_col_offset, eliminate_row_offset = (
            strip_bounds(step_index)
        )
        present = lax.dynamic_slice_in_dim(eliminate_matrix, eliminate_col_offset, PANEL, 1)
        fresh_col = jnp.where(
            (col_id == eliminate_col_owner) & eliminate_active_rows[:, None], left_strip, present
        )
        matrix = lax.dynamic_update_slice_in_dim(
            eliminate_matrix, fresh_col, eliminate_col_offset, 1
        )
        if step_index + 1 < PANELS:
            left_strip, top_strip = (left_next, top_next)
    return matrix[None]


def solution(mesh):
    placed = (
        P("front", None, "row", "column"),
        P("front", None, None),
        P("front", None, None),
        P("front", None),
        P("front", None),
        P("front", None),
        P("front", None, None, None),
    )
    return jax.shard_map(
        body, mesh=mesh, in_specs=placed, out_specs=P("front", "row", "column"), check_vma=False
    )
```
